32 devices in a mesh: dp: 8 (over y, x, core), blk: 4 (over z).
Axes of the slice: x: 2, y: 2, z: 4, core: 2. Of those that a mesh axis runs over, the one named last changes fastest.
Arguments:
- spans: bfloat16 [40960, 1024], P(('dp', 'blk')), may hold values from -6 to 6
- span_counts: int32 [32], P(('dp', 'blk')), may hold values from 16 to 1232, as said below
- session_ids: int32 [40960], P(('dp', 'blk')), may hold values from 0 to 15, as said below
- destinations: int32 [40960], P(('dp', 'blk')), may hold values from 0 to 7, as said below
- expert_weight: bfloat16 [8, 1024, 4096], P('dp'), may hold values from -0.1875 to 0.1875
- norm_gain: float32 [1024], replicated, may hold values from 0.1 to 1.9
- queries: bfloat16 [28672, 4096], P(('dp', 'blk')), may hold values from -6 to 6
- positives: int32 [28672], P(('dp', 'blk')), may hold values from 0 to 63
Outputs:
- loss_rows: float32 [28672], P(('dp', 'blk'))
- grad_queries: bfloat16 [28672, 4096], P(('dp', 'blk'))
- grad_sessions: float32 [512, 4096], P(('dp', 'blk'))
The draws below stay inside these ranges and needn't reach their ends.
Inputs may be any that keep to these rules, and one draw needn't show every extreme that they name: `span_counts`: for each blk index the counts of the devices along dp sum to 2560, and one of them has the largest value. `destinations`: the live rows of the devices that share a blk index, in order of dp index and then of row, name the experts in cyclic order from a drawn start: each expert receives exactly 320 live rows of its blk index, and a device sends at most 154 live rows to one expert, the device with the largest count exactly 154 to each. Rows at or after a device's count name any expert. `session_ids`: on each device the ids of the live rows never fall, begin at 0 and take every value; rows at or after the count carry any id.
All inputs are finite; a program needn't handle non-finite values.
Results may differ from the reference program's by a relative error of at most 0.0072.
Values may be sent and summed in bfloat16 or wider, within the bound.
No kernel may reach another device: no remote copies, remote signals or barrier semaphores. Data moves between devices by JAX's collectives and lax.ppermute only.
A program may use at most 128 MiB of HBM per device.

```python
import jax
import jax.numpy as jnp
from jax import lax

HID = 1024
EMB = 4096
ROWS_DEV = 1280
SESS_DEV = 16
Q_DEV = 896
EXPERTS = 8
SPANS = 40960
SESSIONS = 512
QUERIES = 28672
N_DP = 8
N_BLK = 4


def group_counts(key):
    quad_count = N_DP // 4
    spare_rows = ROWS_DEV - 4 * SESS_DEV
    cut_points = jnp.sort(jax.random.randint(jax.random.fold_in(key, 101), (N_BLK, quad_count, 3), 0, spare_rows + 1), axis=-1)
    pieces = jnp.stack([cut_points[:, :, 0], cut_points[:, :, 1] - cut_points[:, :, 0], cut_points[:, :, 2] - cut_points[:, :, 1], spare_rows - cut_points[:, :, 2]], axis=-1)
    forced = jnp.zeros((N_BLK, 1, 4), jnp.int32).at[:, :, 0].set(spare_rows)
    pieces = jnp.concatenate([forced, pieces[:, 1:, :]], axis=1).reshape(N_BLK, N_DP)
    scores = jax.random.randint(jax.random.fold_in(key, 102), (N_BLK, N_DP), 0, 1 << 20) * N_DP + jnp.arange(N_DP, dtype=jnp.int32)[None, :]
    ordering = jnp.argsort(scores, axis=1).astype(jnp.int32)
    counts = SESS_DEV + jnp.take_along_axis(pieces, ordering, axis=1)
    return jnp.transpose(counts).astype(jnp.int32)


def draw_span_counts(key, part):
    return group_counts(key).reshape(N_DP * N_BLK)


def draw_destinations(key, part):
    counts = group_counts(key)
    starts = jnp.cumsum(counts, axis=0) - counts
    offsets = jax.random.randint(jax.random.fold_in(key, 103), (N_BLK,), 0, N_DP)
    row_index = jnp.arange(ROWS_DEV, dtype=jnp.int32)
    ranking = starts[:, :, None] + offsets[None, :, None] + row_index[None, None, :]
    return (ranking % N_DP).reshape(N_DP * N_BLK * ROWS_DEV).astype(jnp.int32)


def draw_session_ids(key, part):
    counts = group_counts(key)
    row_index = jnp.arange(ROWS_DEV, dtype=jnp.int32)
    raw_scores = jax.random.randint(jax.random.fold_in(key, 104), (N_DP, N_BLK, ROWS_DEV), 0, 1 << 16)
    allowed = (row_index[None, None, :] >= 1) & (row_index[None, None, :] < counts[:, :, None])
    scores = jnp.where(allowed, raw_scores * ROWS_DEV + row_index[None, None, :], -1)
    top_scores, _ = lax.top_k(scores, SESS_DEV - 1)
    cut_points = top_scores % ROWS_DEV
    session_index = jnp.sum((cut_points[:, :, None, :] <= row_index[None, None, :, None]).astype(jnp.int32), axis=-1)
    return session_index.reshape(N_DP * N_BLK * ROWS_DEV).astype(jnp.int32)


def place_ends(array, own_key, low, top_value):
    dims = array.shape
    index_at = [jax.random.randint(jax.random.fold_in(own_key, axis), (), 0, dims[axis]) for axis in range(len(dims))]
    array = array.at[tuple(index_at)].set(low)
    longest = dims.index(max(dims))
    index_at[longest] = (index_at[longest] + 1) % dims[longest]
    return array.at[tuple(index_at)].set(top_value)


def level_of(stream_key, dims, split, smallest, high):
    gain = 1.0
    for dim, shards_of in split:
        heights = jax.random.uniform(jax.random.fold_in(jax.random.fold_in(stream_key, 6), dim), (shards_of,), jnp.float32, smallest / len(split), high / len(split))
        gain = gain * jnp.repeat(jnp.exp(heights), dims[dim] // shards_of).reshape((-1,) + (1,) * (len(dims) - 1 - dim))
    return gain


def bell_draw(rng, extent, width, bound, shards=(), kind=jnp.bfloat16):
    level = level_of(rng, extent, shards, -0.22, 0.18) if shards else 1.0
    drawn = jax.random.normal(rng, extent, jnp.float32) * width * level
    return jnp.minimum(jnp.maximum(drawn, -bound), bound).astype(kind)


def setup_inputs(seed: int = 0) -> dict:
    keys = jax.random.split(jax.random.key(seed), 9)
    return {
        "spans": bell_draw(keys[0], (SPANS, HID), 1.0, 6.0, ((0, 32),)),
        "span_counts": draw_span_counts(jax.random.fold_in(keys[8], 71), 0),
        "session_ids": draw_session_ids(jax.random.fold_in(keys[8], 71), 0),
        "destinations": draw_destinations(jax.random.fold_in(keys[8], 71), 0),
        "expert_weight": bell_draw(keys[4], (EXPERTS, HID, EMB), HID ** -0.5, 0.1875, ((0, 8),)),
        "norm_gain": jnp.clip(1.0 + 0.18 * jax.random.normal(keys[5], (HID,), jnp.float32), 0.1, 1.9),
        "queries": bell_draw(keys[6], (QUERIES, EMB), 1.0, 6.0, ((0, 32),)),
        "positives": place_ends(jax.random.randint(keys[7], (QUERIES,), 0, SESS_DEV * N_BLK), jax.random.fold_in(keys[7], 1), 0, (SESS_DEV * N_BLK) - 1).astype(jnp.int32),
    }


logit_scale = 20.0
epsilon = 1e-06

def unit_rows(values):
    widened = values.astype(jnp.float32)
    return (widened * lax.rsqrt(lax.optimization_barrier(jnp.sum(widened * widened, axis=-1, keepdims=True)) + epsilon)).astype(jnp.bfloat16)

def reference(spans, span_counts, session_ids, destinations, expert_weight, norm_gain, queries, positives):
    group_rows = N_DP * ROWS_DEV
    received = ROWS_DEV // 4
    span_grid = spans.reshape(N_DP, N_BLK, ROWS_DEV, HID)
    count_grid = span_counts.reshape(N_DP, N_BLK)
    session_grid = session_ids.reshape(N_DP, N_BLK, ROWS_DEV)
    target_grid = destinations.reshape(N_DP, N_BLK, ROWS_DEV)
    row_index = jnp.arange(ROWS_DEV, dtype=jnp.int32)
    flat_index = jnp.arange(group_rows, dtype=jnp.int32)
    source_dev = flat_index // ROWS_DEV

    def encode_group(column):
        block_rows = lax.dynamic_index_in_dim(span_grid, column, 1, keepdims=False).reshape(group_rows, HID)
        counts = lax.dynamic_index_in_dim(count_grid, column, 1, keepdims=False)
        sessions = lax.dynamic_index_in_dim(session_grid, column, 1, keepdims=False).reshape(group_rows)
        targets = lax.dynamic_index_in_dim(target_grid, column, 1, keepdims=False).reshape(group_rows)
        live_rows = (row_index[None, :] < counts[:, None]).reshape(group_rows)
        sort_keys = jnp.where(live_rows, targets * group_rows + flat_index, N_DP * group_rows)
        ordering = jnp.argsort(sort_keys)[:N_DP * received].astype(jnp.int32).reshape(N_DP, received)
        picked = block_rows[ordering].astype(jnp.float32)
        normed = (picked * lax.rsqrt(lax.optimization_barrier(jnp.mean(picked * picked, axis=-1, keepdims=True)) + epsilon) * norm_gain).astype(jnp.bfloat16)

        def project(operands):
            return jax.nn.gelu(jnp.dot(operands[0], operands[1], preferred_element_type=jnp.float32), approximate=True).astype(jnp.bfloat16)
        embedded = lax.map(project, (normed, expert_weight))
        slot_index = (source_dev * SESS_DEV + sessions)[ordering].reshape(N_DP * received)
        pooled = jax.ops.segment_sum(embedded.reshape(N_DP * received, EMB).astype(jnp.float32), slot_index, num_segments=N_DP * SESS_DEV)
        return pooled.reshape(N_DP, SESS_DEV, EMB)
    pooled_all = lax.map(encode_group, jnp.arange(N_BLK, dtype=jnp.int32))
    pooled_all = jnp.transpose(pooled_all, (1, 0, 2, 3)).reshape(N_DP, N_BLK * SESS_DEV, EMB)
    query_groups = queries.reshape(N_DP, N_BLK * Q_DEV, EMB)
    positive_groups = positives.reshape(N_DP, N_BLK * Q_DEV)
    doc_count = N_BLK * SESS_DEV

    def contrast(operands):
        query_block, pooled_block, positive_block = operands
        query_unit = unit_rows(query_block)
        doc_unit = unit_rows(pooled_block)
        logits = logit_scale * jnp.dot(query_unit, doc_unit.T, preferred_element_type=jnp.float32)
        weights = jnp.exp(logits)
        totals = lax.optimization_barrier(jnp.sum(weights, axis=1))
        numerator = jnp.dot(weights.astype(jnp.bfloat16), doc_unit, preferred_element_type=jnp.float32)
        matches = positive_block[:, None] == jnp.arange(doc_count, dtype=jnp.int32)[None, :]
        chosen_logit = lax.optimization_barrier(jnp.sum(jnp.where(matches, logits, 0.0), axis=1))
        chosen_doc = doc_unit[positive_block].astype(jnp.float32)
        loss_rows = jnp.log(totals) - chosen_logit
        grad_query = (logit_scale * (numerator / totals[:, None] - chosen_doc)).astype(jnp.bfloat16)
        coefficient = (weights / totals[:, None] - matches.astype(jnp.float32)).astype(jnp.bfloat16)
        grad_doc = logit_scale * jnp.dot(coefficient.T, query_unit, preferred_element_type=jnp.float32)
        return (loss_rows, grad_query, grad_doc)
    loss_all, grad_query_all, grad_doc_all = lax.map(contrast, (query_groups, pooled_all, positive_groups))
    return (loss_all.reshape(QUERIES), grad_query_all.reshape(QUERIES, EMB), grad_doc_all.reshape(SESSIONS, EMB))
```

```python
import jax
import jax.numpy as jnp
from jax import lax
from jax.sharding import PartitionSpec as P

SESS_DEV = 16


logit_scale = 20.0
epsilon = 1e-06


def unit_rows(values):
    widened = values.astype(jnp.float32)
    return (
        widened * lax.rsqrt(jnp.sum(widened * widened, axis=-1, keepdims=True) + epsilon)
    ).astype(jnp.bfloat16)


def contract_rows(left_side, right_side):
    return lax.dot_general(
        left_side, right_side, (((1,), (1,)), ((), ())), preferred_element_type=jnp.float32
    )


def contract_first(left_side, right_side):
    return lax.dot_general(
        left_side, right_side, (((0,), (0,)), ((), ())), preferred_element_type=jnp.float32
    )


def on_device(
    spans, span_counts, session_ids, destinations, expert_weight, norm_gain, queries, positives
):
    rows_dev = spans.shape[0]
    hidden_width = spans.shape[1]
    groups = lax.axis_size("dp")
    capacity = (rows_dev - 3 * SESS_DEV) // groups
    received = rows_dev // 4
    cycle = rows_dev // groups
    count = span_counts[0]

    lane_of = (jnp.arange(groups, dtype=jnp.int32) - destinations[0]) % groups
    by_lane = spans.reshape(cycle, groups, hidden_width)
    send_rows = jnp.swapaxes(jnp.take(by_lane, lane_of, axis=1), 0, 1)[:, :capacity]
    row_of = lane_of[:, None] + groups * jnp.arange(capacity, dtype=jnp.int32)[None, :]
    ids_by_lane = session_ids.reshape(cycle, groups)
    send_ids = jnp.where(
        row_of < count, jnp.swapaxes(jnp.take(ids_by_lane, lane_of, axis=1), 0, 1)[:, :capacity], -1
    )
    got_rows = lax.all_to_all(send_rows, "dp", split_axis=0, concat_axis=0, tiled=True)
    got_ids = lax.all_to_all(send_ids, "dp", split_axis=0, concat_axis=0, tiled=True)

    got_counts = jnp.sum((got_ids >= 0).astype(jnp.int32), axis=1)
    starts = jnp.cumsum(got_counts) - got_counts
    packed_index = jnp.arange(received, dtype=jnp.int32)
    source_of = (
        jnp.sum((starts[None, :] <= packed_index[:, None]).astype(jnp.int32), axis=1) - 1
    )
    slot_of = source_of * capacity + packed_index - starts[source_of]
    packed_live = packed_index < jnp.sum(got_counts)
    slot_of = jnp.where(packed_live, slot_of, 0)
    packed = got_rows.reshape(groups * capacity, hidden_width)[slot_of]
    packed_key = jnp.where(
        packed_live, source_of * SESS_DEV + got_ids.reshape(groups * capacity)[slot_of], -1
    )

    widened = packed.astype(jnp.float32)
    normed = (
        widened
        * lax.rsqrt(jnp.mean(widened * widened, axis=-1, keepdims=True) + epsilon)
        * norm_gain
    ).astype(jnp.bfloat16)
    embedded = jax.nn.gelu(
        jnp.dot(normed, expert_weight[0], preferred_element_type=jnp.float32), approximate=True
    ).astype(jnp.bfloat16)
    emb_width = embedded.shape[1]
    selector = (
        jnp.arange(groups * SESS_DEV, dtype=jnp.int32)[:, None] == packed_key[None, :]
    ).astype(jnp.bfloat16)
    partial = jnp.dot(selector, embedded, preferred_element_type=jnp.float32)
    pooled = lax.psum_scatter(partial, "dp", scatter_dimension=0, tiled=True)

    doc_unit = unit_rows(pooled)
    query_unit = unit_rows(queries)
    doc_piece = lax.all_gather(doc_unit, "blk", axis=0, tiled=True)
    piece_rows = doc_piece.shape[0]
    logits = logit_scale * contract_rows(query_unit, doc_piece)
    weights = jnp.exp(logits)
    totals = jnp.sum(weights, axis=1)
    numerator = jnp.dot(weights.astype(jnp.bfloat16), doc_piece, preferred_element_type=jnp.float32)
    matches = positives[:, None] == jnp.arange(piece_rows, dtype=jnp.int32)[None, :]
    chosen_logit = jnp.sum(jnp.where(matches, logits, 0.0), axis=1)
    chosen_doc = doc_piece[jnp.clip(positives, 0, piece_rows - 1)].astype(jnp.float32)
    loss_rows = jnp.log(totals) - chosen_logit
    grad_queries = (logit_scale * (numerator / totals[:, None] - chosen_doc)).astype(jnp.bfloat16)
    coefficient = (weights / totals[:, None] - matches.astype(jnp.float32)).astype(jnp.bfloat16)
    grad_part = logit_scale * contract_first(coefficient, query_unit)
    grad_docs = lax.psum_scatter(grad_part, "blk", scatter_dimension=0, tiled=True)
    return (loss_rows, grad_queries, grad_docs)


def solution(mesh):
    placed = (
        P(("dp", "blk"), None),
        P(("dp", "blk")),
        P(("dp", "blk")),
        P(("dp", "blk")),
        P("dp", None, None),
        P(),
        P(("dp", "blk"), None),
        P(("dp", "blk")),
    )
    return jax.shard_map(
        on_device,
        mesh=mesh,
        in_specs=placed,
        out_specs=(P(("dp", "blk")), P(("dp", "blk"), None), P(("dp", "blk"), None)),
        check_vma=False,
    )
```

```python
import jax
import jax.numpy as jnp
from jax import lax
from jax.sharding import PartitionSpec as P

SESS_DEV = 16


logit_scale = 20.0
epsilon = 1e-06


def unit_rows(values):
    widened = values.astype(jnp.float32)
    return (
        widened * lax.rsqrt(jnp.sum(widened * widened, axis=-1, keepdims=True) + epsilon)
    ).astype(jnp.bfloat16)


def contract_rows(left_side, right_side):
    return lax.dot_general(
        left_side, right_side, (((1,), (1,)), ((), ())), preferred_element_type=jnp.float32
    )


def contract_first(left_side, right_side):
    return lax.dot_general(
        left_side, right_side, (((0,), (0,)), ((), ())), preferred_element_type=jnp.float32
    )


def on_device(
    spans, span_counts, session_ids, destinations, expert_weight, norm_gain, queries, positives
):
    rows_dev = spans.shape[0]
    hidden_width = spans.shape[1]
    groups = lax.axis_size("dp")
    capacity = (rows_dev - 3 * SESS_DEV) // groups
    received = rows_dev // 4
    cycle = rows_dev // groups
    count = span_counts[0]

    lane_of = (jnp.arange(groups, dtype=jnp.int32) - destinations[0]) % groups
    by_lane = spans.reshape(cycle, groups, hidden_width)
    send_rows = jnp.swapaxes(jnp.take(by_lane, lane_of, axis=1), 0, 1)[:, :capacity]
    row_of = lane_of[:, None] + groups * jnp.arange(capacity, dtype=jnp.int32)[None, :]
    ids_by_lane = session_ids.reshape(cycle, groups)
    send_ids = jnp.where(
        row_of < count, jnp.swapaxes(jnp.take(ids_by_lane, lane_of, axis=1), 0, 1)[:, :capacity], -1
    )
    got_rows = lax.all_to_all(send_rows, "dp", split_axis=0, concat_axis=0, tiled=True)
    got_ids = lax.all_to_all(send_ids, "dp", split_axis=0, concat_axis=0, tiled=True)

    got_counts = jnp.sum((got_ids >= 0).astype(jnp.int32), axis=1)
    starts = jnp.cumsum(got_counts) - got_counts
    packed_index = jnp.arange(received, dtype=jnp.int32)
    source_of = (
        jnp.sum((starts[None, :] <= packed_index[:, None]).astype(jnp.int32), axis=1) - 1
    )
    slot_of = source_of * capacity + packed_index - starts[source_of]
    packed_live = packed_index < jnp.sum(got_counts)
    slot_of = jnp.where(packed_live, slot_of, 0)
    packed = got_rows.reshape(groups * capacity, hidden_width)[slot_of]
    packed_key = jnp.where(
        packed_live, source_of * SESS_DEV + got_ids.reshape(groups * capacity)[slot_of], -1
    )

    widened = packed.astype(jnp.float32)
    normed = (
        widened
        * lax.rsqrt(jnp.mean(widened * widened, axis=-1, keepdims=True) + epsilon)
        * norm_gain
    ).astype(jnp.bfloat16)
    embedded = jax.nn.gelu(
        jnp.dot(normed, expert_weight[0], preferred_element_type=jnp.float32), approximate=True
    ).astype(jnp.bfloat16)
    emb_width = embedded.shape[1]
    selector = (
        jnp.arange(groups * SESS_DEV, dtype=jnp.int32)[:, None] == packed_key[None, :]
    ).astype(jnp.bfloat16)
    partial = jnp.dot(selector, embedded, preferred_element_type=jnp.float32)
    partial = partial.astype(jnp.bfloat16).reshape(groups, SESS_DEV, emb_width)
    returned = lax.all_to_all(partial, "dp", split_axis=0, concat_axis=0, tiled=True)
    pooled = jnp.sum(returned.astype(jnp.float32), axis=0)

    doc_unit = unit_rows(pooled)
    query_unit = unit_rows(queries)
    doc_piece = lax.all_gather(doc_unit, "blk", axis=0, tiled=True)
    piece_rows = doc_piece.shape[0]
    logits = logit_scale * contract_rows(query_unit, doc_piece)
    weights = jnp.exp(logits)
    totals = jnp.sum(weights, axis=1)
    numerator = jnp.dot(weights.astype(jnp.bfloat16), doc_piece, preferred_element_type=jnp.float32)
    matches = positives[:, None] == jnp.arange(piece_rows, dtype=jnp.int32)[None, :]
    chosen_logit = jnp.sum(jnp.where(matches, logits, 0.0), axis=1)
    chosen_doc = jnp.dot(
        matches.astype(jnp.bfloat16), doc_piece, preferred_element_type=jnp.float32
    )
    loss_rows = jnp.log(totals) - chosen_logit
    grad_queries = (logit_scale * (numerator / totals[:, None] - chosen_doc)).astype(jnp.bfloat16)
    coefficient = (weights / totals[:, None] - matches.astype(jnp.float32)).astype(jnp.bfloat16)
    grad_part = logit_scale * contract_first(coefficient, query_unit)
    grad_docs = lax.psum_scatter(grad_part, "blk", scatter_dimension=0, tiled=True)
    return (loss_rows, grad_queries, grad_docs)


def solution(mesh):
    placed = (
        P(("dp", "blk"), None),
        P(("dp", "blk")),
        P(("dp", "blk")),
        P(("dp", "blk")),
        P("dp", None, None),
        P(),
        P(("dp", "blk"), None),
        P(("dp", "blk")),
    )
    return jax.shard_map(
        on_device,
        mesh=mesh,
        in_specs=placed,
        out_specs=(P(("dp", "blk")), P(("dp", "blk"), None), P(("dp", "blk"), None)),
        check_vma=False,
    )
```

```python
import jax
import jax.numpy as jnp
from jax import lax
from jax.sharding import PartitionSpec as P

SESS_DEV = 16


logit_scale = 20.0
epsilon = 1e-06


def unit_rows(values):
    widened = values.astype(jnp.float32)
    return (
        widened * lax.rsqrt(jnp.sum(widened * widened, axis=-1, keepdims=True) + epsilon)
    ).astype(jnp.bfloat16)


def contract_rows(left_side, right_side):
    return lax.dot_general(
        left_side, right_side, (((1,), (1,)), ((), ())), preferred_element_type=jnp.float32
    )


def contract_first(left_side, right_side):
    return lax.dot_general(
        left_side, right_side, (((0,), (0,)), ((), ())), preferred_element_type=jnp.float32
    )


def on_device(
    spans, span_counts, session_ids, destinations, expert_weight, norm_gain, queries, positives
):
    rows_dev = spans.shape[0]
    hidden_width = spans.shape[1]
    groups = lax.axis_size("dp")
    capacity = (rows_dev - 3 * SESS_DEV) // groups
    received = rows_dev // 4
    count = span_counts[0]

    lane_of = (jnp.arange(groups, dtype=jnp.int32) - destinations[0]) % groups
    row_of = lane_of[:, None] + groups * jnp.arange(capacity, dtype=jnp.int32)[None, :]
    send_rows = spans[row_of.reshape(groups * capacity)].reshape(groups, capacity, hidden_width)
    tag = jnp.where(row_of < count, session_ids[row_of] + 1, 0).astype(jnp.bfloat16)
    tag_row = jnp.zeros((groups, 1, hidden_width), jnp.bfloat16).at[:, 0, :capacity].set(tag)
    send = jnp.concatenate([send_rows, tag_row], axis=1)
    got = lax.all_to_all(send, "dp", split_axis=0, concat_axis=0, tiled=True)
    block = capacity + 1
    got_ids = got[:, capacity, :capacity].astype(jnp.int32) - 1

    got_counts = jnp.sum((got_ids >= 0).astype(jnp.int32), axis=1)
    starts = jnp.cumsum(got_counts) - got_counts
    packed_index = jnp.arange(received, dtype=jnp.int32)
    source_of = (
        jnp.sum((starts[None, :] <= packed_index[:, None]).astype(jnp.int32), axis=1) - 1
    )
    rank_of = packed_index - starts[source_of]
    packed_live = packed_index < jnp.sum(got_counts)
    rank_of = jnp.where(packed_live, rank_of, 0)
    packed = got.reshape(groups * block, hidden_width)[source_of * block + rank_of]
    packed_key = jnp.where(
        packed_live, source_of * SESS_DEV + got_ids.reshape(groups * capacity)[source_of * capacity + rank_of], -1
    )

    widened = packed.astype(jnp.float32)
    normed = (
        widened
        * lax.rsqrt(jnp.mean(widened * widened, axis=-1, keepdims=True) + epsilon)
        * norm_gain
    ).astype(jnp.bfloat16)
    embedded = jax.nn.gelu(
        jnp.dot(normed, expert_weight[0], preferred_element_type=jnp.float32), approximate=True
    ).astype(jnp.bfloat16)
    emb_width = embedded.shape[1]
    selector = (
        jnp.arange(groups * SESS_DEV, dtype=jnp.int32)[:, None] == packed_key[None, :]
    ).astype(jnp.bfloat16)
    partial = jnp.dot(selector, embedded, preferred_element_type=jnp.float32)
    partial = partial.astype(jnp.bfloat16).reshape(groups, SESS_DEV, emb_width)
    returned = lax.all_to_all(partial, "dp", split_axis=0, concat_axis=0, tiled=True)
    pooled = jnp.sum(returned.astype(jnp.float32), axis=0)

    doc_unit = unit_rows(pooled)
    query_unit = unit_rows(queries)
    cycle_size = lax.axis_size("blk")
    position = lax.axis_index("blk")
    arrived = [doc_unit] + [
        lax.ppermute(doc_unit, "blk", [(i, (i + shift) % cycle_size) for i in range(cycle_size)])
        for shift in range(1, cycle_size)
    ]
    stacked = jnp.stack(arrived)
    source_order = (position - jnp.arange(cycle_size, dtype=jnp.int32)) % cycle_size
    doc_piece = jnp.zeros_like(stacked).at[source_order].set(stacked).reshape(
        cycle_size * doc_unit.shape[0], doc_unit.shape[1]
    )
    piece_rows = doc_piece.shape[0]
    logits = logit_scale * contract_rows(query_unit, doc_piece)
    weights = jnp.exp(logits)
    totals = jnp.sum(weights, axis=1)
    numerator = jnp.dot(weights.astype(jnp.bfloat16), doc_piece, preferred_element_type=jnp.float32)
    matches = positives[:, None] == jnp.arange(piece_rows, dtype=jnp.int32)[None, :]
    chosen_logit = jnp.sum(jnp.where(matches, logits, 0.0), axis=1)
    chosen_doc = jnp.dot(
        matches.astype(jnp.bfloat16), doc_piece, preferred_element_type=jnp.float32
    )
    loss_rows = jnp.log(totals) - chosen_logit
    grad_queries = (logit_scale * (numerator / totals[:, None] - chosen_doc)).astype(jnp.bfloat16)
    coefficient = (weights / totals[:, None] - matches.astype(jnp.float32)).astype(jnp.bfloat16)
    grad_part = logit_scale * contract_first(coefficient, query_unit)
    grad_terms = lax.all_to_all(
        grad_part.reshape(cycle_size, doc_unit.shape[0], emb_width), "blk", split_axis=0, concat_axis=0, tiled=True
    )
    grad_docs = jnp.sum(grad_terms, axis=0)
    return (loss_rows, grad_queries, grad_docs)


def solution(mesh):
    placed = (
        P(("dp", "blk"), None),
        P(("dp", "blk")),
        P(("dp", "blk")),
        P(("dp", "blk")),
        P("dp", None, None),
        P(),
        P(("dp", "blk"), None),
        P(("dp", "blk")),
    )
    return jax.shard_map(
        on_device,
        mesh=mesh,
        in_specs=placed,
        out_specs=(P(("dp", "blk")), P(("dp", "blk"), None), P(("dp", "blk"), None)),
        check_vma=False,
    )
```

```python
import jax
import jax.numpy as jnp
from jax import lax
from jax.experimental import pallas as pl
from jax.experimental.pallas import tpu as pltpu
from jax.sharding import PartitionSpec as P

SESS_DEV = 16


logit_scale = 20.0
epsilon = 1e-06


def unit_rows(values):
    widened = values.astype(jnp.float32)
    return (
        widened * lax.rsqrt(jnp.sum(widened * widened, axis=-1, keepdims=True) + epsilon)
    ).astype(jnp.bfloat16)


def contract_rows(left_side, right_side):
    return lax.dot_general(
        left_side, right_side, (((1,), (1,)), ((), ())), preferred_element_type=jnp.float32
    )


def contract_first(left_side, right_side):
    return lax.dot_general(
        left_side, right_side, (((0,), (0,)), ((), ())), preferred_element_type=jnp.float32
    )


def contrast_kernel(q_ref, d_ref, pos_ref, loss_ref, gq_ref, gd_ref):
    @pl.when(pl.program_id(0) == 0)
    def _():
        gd_ref[...] = jnp.zeros_like(gd_ref)

    widened = q_ref[...].astype(jnp.float32)
    query_unit = (
        widened * lax.rsqrt(jnp.sum(widened * widened, axis=-1, keepdims=True) + epsilon)
    ).astype(jnp.bfloat16)
    docs = d_ref[...]
    logits = logit_scale * contract_rows(query_unit, docs)
    weights = jnp.exp(logits)
    totals = jnp.sum(weights, axis=1, keepdims=True)
    numerator = jnp.dot(weights.astype(jnp.bfloat16), docs, preferred_element_type=jnp.float32)
    matches = pos_ref[...] == lax.broadcasted_iota(jnp.int32, logits.shape, 1)
    hits = matches.astype(jnp.float32)
    chosen_logit = jnp.sum(jnp.where(matches, logits, 0.0), axis=1, keepdims=True)
    chosen_doc = jnp.dot(hits.astype(jnp.bfloat16), docs, preferred_element_type=jnp.float32)
    loss_ref[...] = jnp.log(totals) - chosen_logit
    gq_ref[...] = (logit_scale * (numerator / totals - chosen_doc)).astype(jnp.bfloat16)
    coefficient_t = (weights / totals - hits).T.astype(jnp.bfloat16)
    gd_ref[...] += logit_scale * jnp.dot(
        coefficient_t, query_unit, preferred_element_type=jnp.float32
    )


def contrast(queries, doc_piece, positives, tile=128):
    rows, width = queries.shape
    docs = doc_piece.shape[0]
    steps = rows // tile
    return pl.pallas_call(
        contrast_kernel,
        grid=(steps,),
        in_specs=[
            pl.BlockSpec((tile, width), lambda i: (i, 0)),
            pl.BlockSpec((docs, width), lambda i: (0, 0)),
            pl.BlockSpec((tile, 1), lambda i: (i, 0)),
        ],
        out_specs=[
            pl.BlockSpec((tile, 1), lambda i: (i, 0)),
            pl.BlockSpec((tile, width), lambda i: (i, 0)),
            pl.BlockSpec((docs, width), lambda i: (0, 0)),
        ],
        out_shape=[
            jax.ShapeDtypeStruct((rows, 1), jnp.float32),
            jax.ShapeDtypeStruct((rows, width), jnp.bfloat16),
            jax.ShapeDtypeStruct((docs, width), jnp.float32),
        ],
        compiler_params=pltpu.CompilerParams(dimension_semantics=("arbitrary",)),
        cost_estimate=pl.CostEstimate(
            flops=8 * rows * docs * width, transcendentals=rows * docs, bytes_accessed=4 * rows * width
        ),
    )(queries, doc_piece, positives.reshape(rows, 1))


def on_device(
    spans, span_counts, session_ids, destinations, expert_weight, norm_gain, queries, positives
):
    rows_dev = spans.shape[0]
    hidden_width = spans.shape[1]
    groups = lax.axis_size("dp")
    capacity = (rows_dev - 3 * SESS_DEV) // groups
    received = rows_dev // 4
    cycle = rows_dev // groups
    count = span_counts[0]

    lane_of = (jnp.arange(groups, dtype=jnp.int32) - destinations[0]) % groups
    by_lane = spans.reshape(cycle, groups, hidden_width)
    send_rows = jnp.swapaxes(jnp.take(by_lane, lane_of, axis=1), 0, 1)[:, :capacity]
    row_of = lane_of[:, None] + groups * jnp.arange(capacity, dtype=jnp.int32)[None, :]
    ids_by_lane = session_ids.reshape(cycle, groups)
    send_ids = jnp.where(
        row_of < count, jnp.swapaxes(jnp.take(ids_by_lane, lane_of, axis=1), 0, 1)[:, :capacity], -1
    )
    got_rows = lax.all_to_all(send_rows, "dp", split_axis=0, concat_axis=0, tiled=True)
    got_ids = lax.all_to_all(send_ids, "dp", split_axis=0, concat_axis=0, tiled=True)

    got_counts = jnp.sum((got_ids >= 0).astype(jnp.int32), axis=1)
    starts = jnp.cumsum(got_counts) - got_counts
    packed_index = jnp.arange(received, dtype=jnp.int32)
    source_of = (
        jnp.sum((starts[None, :] <= packed_index[:, None]).astype(jnp.int32), axis=1) - 1
    )
    slot_of = source_of * capacity + packed_index - starts[source_of]
    packed_live = packed_index < jnp.sum(got_counts)
    slot_of = jnp.where(packed_live, slot_of, 0)
    packed = got_rows.reshape(groups * capacity, hidden_width)[slot_of]
    packed_key = jnp.where(
        packed_live, source_of * SESS_DEV + got_ids.reshape(groups * capacity)[slot_of], -1
    )

    widened = packed.astype(jnp.float32)
    normed = (
        widened
        * lax.rsqrt(jnp.mean(widened * widened, axis=-1, keepdims=True) + epsilon)
        * norm_gain
    ).astype(jnp.bfloat16)
    embedded = jax.nn.gelu(
        jnp.dot(normed, expert_weight[0], preferred_element_type=jnp.float32), approximate=True
    ).astype(jnp.bfloat16)
    emb_width = embedded.shape[1]
    selector = (
        jnp.arange(groups * SESS_DEV, dtype=jnp.int32)[:, None] == packed_key[None, :]
    ).astype(jnp.bfloat16)
    partial = jnp.dot(selector, embedded, preferred_element_type=jnp.float32)
    partial = partial.astype(jnp.bfloat16).reshape(groups, SESS_DEV, emb_width)
    returned = lax.all_to_all(partial, "dp", split_axis=0, concat_axis=0, tiled=True)
    pooled = jnp.sum(returned.astype(jnp.float32), axis=0)

    doc_unit = unit_rows(pooled)
    cycle_size = lax.axis_size("blk")
    position = lax.axis_index("blk")
    arrived = jnp.stack(
        [doc_unit]
        + [
            lax.ppermute(doc_unit, "blk", [(i, (i + shift) % cycle_size) for i in range(cycle_size)])
            for shift in range(1, cycle_size)
        ]
    )
    arrival_of = (position - jnp.arange(cycle_size, dtype=jnp.int32)) % cycle_size
    doc_piece = arrived[arrival_of].reshape(cycle_size * doc_unit.shape[0], emb_width)
    loss_col, grad_queries, grad_part = contrast(queries, doc_piece, positives)
    loss_rows = loss_col.reshape(loss_col.shape[0])
    grad_docs = lax.psum_scatter(grad_part, "blk", scatter_dimension=0, tiled=True)
    return (loss_rows, grad_queries, grad_docs)


def solution(mesh):
    placed = (
        P(("dp", "blk"), None),
        P(("dp", "blk")),
        P(("dp", "blk")),
        P(("dp", "blk")),
        P("dp", None, None),
        P(),
        P(("dp", "blk"), None),
        P(("dp", "blk")),
    )
    return jax.shard_map(
        on_device,
        mesh=mesh,
        in_specs=placed,
        out_specs=(P(("dp", "blk")), P(("dp", "blk"), None), P(("dp", "blk"), None)),
        check_vma=False,
    )
```

```python
import jax
import jax.numpy as jnp
from jax import lax
from jax.experimental import pallas as pl
from jax.experimental.pallas import tpu as pltpu
from jax.sharding import PartitionSpec as P

SESS_DEV = 16


logit_scale = 20.0
epsilon = 1e-06


def unit_rows(values):
    widened = values.astype(jnp.float32)
    return (
        widened * lax.rsqrt(jnp.sum(widened * widened, axis=-1, keepdims=True) + epsilon)
    ).astype(jnp.bfloat16)


def contract_rows(left_side, right_side):
    return lax.dot_general(
        left_side, right_side, (((1,), (1,)), ((), ())), preferred_element_type=jnp.float32
    )


def contract_first(left_side, right_side):
    return lax.dot_general(
        left_side, right_side, (((0,), (0,)), ((), ())), preferred_element_type=jnp.float32
    )


def score_kernel(q_ref, d_ref, hit_ref, loss_ref, wb_ref, tot_ref, gd_ref):
    @pl.when(pl.program_id(0) == 0)
    def _():
        gd_ref[...] = jnp.zeros_like(gd_ref)

    widened = q_ref[...].astype(jnp.float32)
    query_unit = (
        widened * lax.rsqrt(jnp.sum(widened * widened, axis=-1, keepdims=True) + epsilon)
    ).astype(jnp.bfloat16)
    logits = logit_scale * contract_rows(query_unit, d_ref[...])
    weights = jnp.exp(logits)
    totals = jnp.sum(weights, axis=1, keepdims=True)
    hits = hit_ref[...].astype(jnp.float32)
    chosen_logit = jnp.sum(hits * logits, axis=1, keepdims=True)
    loss_ref[...] = jnp.log(totals) - chosen_logit
    wb_ref[...] = weights.astype(jnp.bfloat16)
    tot_ref[...] = totals
    coefficient_t = (weights / totals - hits).T.astype(jnp.bfloat16)
    gd_ref[...] += logit_scale * jnp.dot(
        coefficient_t, query_unit, preferred_element_type=jnp.float32
    )


def query_grad_kernel(wb_ref, tot_ref, hit_ref, d_ref, gq_ref):
    docs = d_ref[...]
    numerator = jnp.dot(wb_ref[...], docs, preferred_element_type=jnp.float32)
    chosen_doc = jnp.dot(hit_ref[...], docs, preferred_element_type=jnp.float32)
    gq_ref[...] = (logit_scale * (numerator / tot_ref[...] - chosen_doc)).astype(jnp.bfloat16)


def scores(queries, doc_piece, hits, tile=128):
    rows, width = queries.shape
    docs = doc_piece.shape[0]
    return pl.pallas_call(
        score_kernel,
        grid=(rows // tile,),
        in_specs=[
            pl.BlockSpec((tile, width), lambda i: (i, 0)),
            pl.BlockSpec((docs, width), lambda i: (0, 0)),
            pl.BlockSpec((tile, docs), lambda i: (i, 0)),
        ],
        out_specs=[
            pl.BlockSpec((tile, 1), lambda i: (i, 0)),
            pl.BlockSpec((tile, docs), lambda i: (i, 0)),
            pl.BlockSpec((tile, 1), lambda i: (i, 0)),
            pl.BlockSpec((docs, width), lambda i: (0, 0)),
        ],
        out_shape=[
            jax.ShapeDtypeStruct((rows, 1), jnp.float32),
            jax.ShapeDtypeStruct((rows, docs), jnp.bfloat16),
            jax.ShapeDtypeStruct((rows, 1), jnp.float32),
            jax.ShapeDtypeStruct((docs, width), jnp.float32),
        ],
        compiler_params=pltpu.CompilerParams(dimension_semantics=("arbitrary",)),
        cost_estimate=pl.CostEstimate(
            flops=4 * rows * docs * width, transcendentals=rows * docs, bytes_accessed=2 * rows * width
        ),
    )(queries, doc_piece, hits)


def query_grads(weights, totals, hits, doc_piece, tile=128):
    rows, docs = weights.shape
    width = doc_piece.shape[1]
    return pl.pallas_call(
        query_grad_kernel,
        grid=(rows // tile,),
        in_specs=[
            pl.BlockSpec((tile, docs), lambda i: (i, 0)),
            pl.BlockSpec((tile, 1), lambda i: (i, 0)),
            pl.BlockSpec((tile, docs), lambda i: (i, 0)),
            pl.BlockSpec((docs, width), lambda i: (0, 0)),
        ],
        out_specs=pl.BlockSpec((tile, width), lambda i: (i, 0)),
        out_shape=jax.ShapeDtypeStruct((rows, width), jnp.bfloat16),
        compiler_params=pltpu.CompilerParams(dimension_semantics=("arbitrary",)),
        cost_estimate=pl.CostEstimate(
            flops=4 * rows * docs * width, transcendentals=0, bytes_accessed=2 * rows * width
        ),
    )(weights, totals, hits, doc_piece)


def on_device(
    spans, span_counts, session_ids, destinations, expert_weight, norm_gain, queries, positives
):
    rows_dev = spans.shape[0]
    hidden_width = spans.shape[1]
    groups = lax.axis_size("dp")
    capacity = (rows_dev - 3 * SESS_DEV) // groups
    received = rows_dev // 4
    cycle = rows_dev // groups
    count = span_counts[0]

    lane_of = (jnp.arange(groups, dtype=jnp.int32) - destinations[0]) % groups
    by_lane = spans.reshape(cycle, groups, hidden_width)
    send_rows = jnp.swapaxes(jnp.take(by_lane, lane_of, axis=1), 0, 1)[:, :capacity]
    row_of = lane_of[:, None] + groups * jnp.arange(capacity, dtype=jnp.int32)[None, :]
    ids_by_lane = session_ids.reshape(cycle, groups)
    send_ids = jnp.where(
        row_of < count, jnp.swapaxes(jnp.take(ids_by_lane, lane_of, axis=1), 0, 1)[:, :capacity], -1
    )
    got_rows = lax.all_to_all(send_rows, "dp", split_axis=0, concat_axis=0, tiled=True)
    got_ids = lax.all_to_all(send_ids, "dp", split_axis=0, concat_axis=0, tiled=True)

    got_counts = jnp.sum((got_ids >= 0).astype(jnp.int32), axis=1)
    starts = jnp.cumsum(got_counts) - got_counts
    packed_index = jnp.arange(received, dtype=jnp.int32)
    source_of = (
        jnp.sum((starts[None, :] <= packed_index[:, None]).astype(jnp.int32), axis=1) - 1
    )
    slot_of = source_of * capacity + packed_index - starts[source_of]
    packed_live = packed_index < jnp.sum(got_counts)
    slot_of = jnp.where(packed_live, slot_of, 0)
    packed = got_rows.reshape(groups * capacity, hidden_width)[slot_of]
    packed_key = jnp.where(
        packed_live, source_of * SESS_DEV + got_ids.reshape(groups * capacity)[slot_of], -1
    )

    widened = packed.astype(jnp.float32)
    normed = (
        widened
        * lax.rsqrt(jnp.mean(widened * widened, axis=-1, keepdims=True) + epsilon)
        * norm_gain
    ).astype(jnp.bfloat16)
    embedded = jax.nn.gelu(
        jnp.dot(normed, expert_weight[0], preferred_element_type=jnp.float32), approximate=True
    ).astype(jnp.bfloat16)
    emb_width = embedded.shape[1]
    selector = (
        jnp.arange(groups * SESS_DEV, dtype=jnp.int32)[:, None] == packed_key[None, :]
    ).astype(jnp.bfloat16)
    partial = jnp.dot(selector, embedded, preferred_element_type=jnp.float32)
    partial = partial.astype(jnp.bfloat16).reshape(groups, SESS_DEV, emb_width)
    returned = lax.all_to_all(partial, "dp", split_axis=0, concat_axis=0, tiled=True)
    pooled = jnp.sum(returned.astype(jnp.float32), axis=0)

    doc_unit = unit_rows(pooled)
    cycle_size = lax.axis_size("blk")
    position = lax.axis_index("blk")
    arrived = jnp.stack(
        [doc_unit]
        + [
            lax.ppermute(doc_unit, "blk", [(i, (i + shift) % cycle_size) for i in range(cycle_size)])
            for shift in range(1, cycle_size)
        ]
    )
    arrival_of = (position - jnp.arange(cycle_size, dtype=jnp.int32)) % cycle_size
    doc_piece = arrived[arrival_of].reshape(cycle_size * doc_unit.shape[0], emb_width)
    piece_rows = doc_piece.shape[0]
    hits = (positives[:, None] == jnp.arange(piece_rows, dtype=jnp.int32)[None, :]).astype(
        jnp.bfloat16
    )
    loss_col, weights, totals, grad_part = scores(queries, doc_piece, hits)
    grad_docs = lax.psum_scatter(grad_part, "blk", scatter_dimension=0, tiled=True)
    grad_queries = query_grads(weights, totals, hits, doc_piece)
    loss_rows = loss_col.reshape(loss_col.shape[0])
    return (loss_rows, grad_queries, grad_docs)


def solution(mesh):
    placed = (
        P(("dp", "blk"), None),
        P(("dp", "blk")),
        P(("dp", "blk")),
        P(("dp", "blk")),
        P("dp", None, None),
        P(),
        P(("dp", "blk"), None),
        P(("dp", "blk")),
    )
    return jax.shard_map(
        on_device,
        mesh=mesh,
        in_specs=placed,
        out_specs=(P(("dp", "blk")), P(("dp", "blk"), None), P(("dp", "blk"), None)),
        check_vma=False,
    )
```

```python
import jax
import jax.numpy as jnp
from jax import lax
from jax.experimental import pallas as pl
from jax.experimental.pallas import tpu as pltpu
from jax.sharding import PartitionSpec as P

SESS_DEV = 16


logit_scale = 20.0
epsilon = 1e-06


def unit_rows(values):
    widened = values.astype(jnp.float32)
    return (
        widened * lax.rsqrt(jnp.sum(widened * widened, axis=-1, keepdims=True) + epsilon)
    ).astype(jnp.bfloat16)


def contract_rows(left_side, right_side):
    return lax.dot_general(
        left_side, right_side, (((1,), (1,)), ((), ())), preferred_element_type=jnp.float32
    )


def contract_first(left_side, right_side):
    return lax.dot_general(
        left_side, right_side, (((0,), (0,)), ((), ())), preferred_element_type=jnp.float32
    )


def score_kernel(q_ref, d_ref, hit_ref, loss_ref, wb_ref, tot_ref, gd_ref):
    @pl.when(pl.program_id(0) == 0)
    def _():
        gd_ref[...] = jnp.zeros_like(gd_ref)

    widened = q_ref[...].astype(jnp.float32)
    query_unit = (
        widened * lax.rsqrt(jnp.sum(widened * widened, axis=-1, keepdims=True) + epsilon)
    ).astype(jnp.bfloat16)
    logits = logit_scale * contract_rows(query_unit, d_ref[...])
    weights = jnp.exp(logits)
    totals = jnp.sum(weights, axis=1, keepdims=True)
    hits = hit_ref[...].astype(jnp.float32)
    chosen_logit = jnp.sum(hits * logits, axis=1, keepdims=True)
    loss_ref[...] = jnp.log(totals) - chosen_logit
    wb_ref[...] = weights.astype(jnp.bfloat16)
    tot_ref[...] = totals
    coefficient_t = (weights / totals - hits).T.astype(jnp.bfloat16)
    gd_ref[...] += logit_scale * jnp.dot(
        coefficient_t, query_unit, preferred_element_type=jnp.float32
    )


def query_grad_kernel(wb_ref, tot_ref, hit_ref, d_ref, gq_ref):
    docs = d_ref[...]
    numerator = jnp.dot(wb_ref[...], docs, preferred_element_type=jnp.float32)
    chosen_doc = jnp.dot(hit_ref[...], docs, preferred_element_type=jnp.float32)
    gq_ref[...] = (logit_scale * (numerator / tot_ref[...] - chosen_doc)).astype(jnp.bfloat16)


def scores(queries, doc_piece, hits, tile=128):
    rows, width = queries.shape
    docs = doc_piece.shape[0]
    return pl.pallas_call(
        score_kernel,
        grid=(rows // tile,),
        in_specs=[
            pl.BlockSpec((tile, width), lambda i: (i, 0)),
            pl.BlockSpec((docs, width), lambda i: (0, 0)),
            pl.BlockSpec((tile, docs), lambda i: (i, 0)),
        ],
        out_specs=[
            pl.BlockSpec((tile, 1), lambda i: (i, 0)),
            pl.BlockSpec((tile, docs), lambda i: (i, 0)),
            pl.BlockSpec((tile, 1), lambda i: (i, 0)),
            pl.BlockSpec((docs, width), lambda i: (0, 0)),
        ],
        out_shape=[
            jax.ShapeDtypeStruct((rows, 1), jnp.float32),
            jax.ShapeDtypeStruct((rows, docs), jnp.bfloat16),
            jax.ShapeDtypeStruct((rows, 1), jnp.float32),
            jax.ShapeDtypeStruct((docs, width), jnp.float32),
        ],
        compiler_params=pltpu.CompilerParams(dimension_semantics=("arbitrary",)),
        cost_estimate=pl.CostEstimate(
            flops=4 * rows * docs * width, transcendentals=rows * docs, bytes_accessed=2 * rows * width
        ),
    )(queries, doc_piece, hits)


def query_grads(weights, totals, hits, doc_piece, tile=128):
    rows, docs = weights.shape
    width = doc_piece.shape[1]
    return pl.pallas_call(
        query_grad_kernel,
        grid=(rows // tile,),
        in_specs=[
            pl.BlockSpec((tile, docs), lambda i: (i, 0)),
            pl.BlockSpec((tile, 1), lambda i: (i, 0)),
            pl.BlockSpec((tile, docs), lambda i: (i, 0)),
            pl.BlockSpec((docs, width), lambda i: (0, 0)),
        ],
        out_specs=pl.BlockSpec((tile, width), lambda i: (i, 0)),
        out_shape=jax.ShapeDtypeStruct((rows, width), jnp.bfloat16),
        compiler_params=pltpu.CompilerParams(dimension_semantics=("arbitrary",)),
        cost_estimate=pl.CostEstimate(
            flops=4 * rows * docs * width, transcendentals=0, bytes_accessed=2 * rows * width
        ),
    )(weights, totals, hits, doc_piece)


def line_reduce_scatter(parts, axis):
    size = lax.axis_size(axis)
    own = lax.axis_index(axis)
    rightward = [(i, i + 1) for i in range(size - 1)]
    leftward = [(i + 1, i) for i in range(size - 1)]
    from_left = jnp.zeros_like(parts[0])
    from_right = jnp.zeros_like(parts[0])
    for step in range(1, size):
        right_block = jnp.minimum(own + (size - step), size - 1)
        left_block = jnp.maximum(own - (size - step), 0)
        from_left = lax.ppermute(parts[right_block] + from_left, axis, rightward)
        from_right = lax.ppermute(parts[left_block] + from_right, axis, leftward)
    return parts[own] + from_left + from_right


def on_device(
    spans, span_counts, session_ids, destinations, expert_weight, norm_gain, queries, positives
):
    rows_dev = spans.shape[0]
    hidden_width = spans.shape[1]
    groups = lax.axis_size("dp")
    capacity = (rows_dev - 3 * SESS_DEV) // groups
    received = rows_dev // 4
    cycle = rows_dev // groups
    count = span_counts[0]

    lane_of = (jnp.arange(groups, dtype=jnp.int32) - destinations[0]) % groups
    by_lane = spans.reshape(cycle, groups, hidden_width)
    send_rows = jnp.swapaxes(jnp.take(by_lane, lane_of, axis=1), 0, 1)[:, :capacity]
    row_of = lane_of[:, None] + groups * jnp.arange(capacity, dtype=jnp.int32)[None, :]
    ids_by_lane = session_ids.reshape(cycle, groups)
    send_ids = jnp.where(
        row_of < count, jnp.swapaxes(jnp.take(ids_by_lane, lane_of, axis=1), 0, 1)[:, :capacity], -1
    )
    got_rows = lax.all_to_all(send_rows, "dp", split_axis=0, concat_axis=0, tiled=True)
    got_ids = lax.all_to_all(send_ids, "dp", split_axis=0, concat_axis=0, tiled=True)

    got_counts = jnp.sum((got_ids >= 0).astype(jnp.int32), axis=1)
    starts = jnp.cumsum(got_counts) - got_counts
    packed_index = jnp.arange(received, dtype=jnp.int32)
    source_of = (
        jnp.sum((starts[None, :] <= packed_index[:, None]).astype(jnp.int32), axis=1) - 1
    )
    slot_of = source_of * capacity + packed_index - starts[source_of]
    packed_live = packed_index < jnp.sum(got_counts)
    slot_of = jnp.where(packed_live, slot_of, 0)
    packed = got_rows.reshape(groups * capacity, hidden_width)[slot_of]
    packed_key = jnp.where(
        packed_live, source_of * SESS_DEV + got_ids.reshape(groups * capacity)[slot_of], -1
    )

    widened = packed.astype(jnp.float32)
    normed = (
        widened
        * lax.rsqrt(jnp.mean(widened * widened, axis=-1, keepdims=True) + epsilon)
        * norm_gain
    ).astype(jnp.bfloat16)
    embedded = jax.nn.gelu(
        jnp.dot(normed, expert_weight[0], preferred_element_type=jnp.float32), approximate=True
    ).astype(jnp.bfloat16)
    emb_width = embedded.shape[1]
    selector = (
        jnp.arange(groups * SESS_DEV, dtype=jnp.int32)[:, None] == packed_key[None, :]
    ).astype(jnp.bfloat16)
    partial = jnp.dot(selector, embedded, preferred_element_type=jnp.float32)
    partial = partial.astype(jnp.bfloat16).reshape(groups, SESS_DEV, emb_width)
    returned = lax.all_to_all(partial, "dp", split_axis=0, concat_axis=0, tiled=True)
    pooled = jnp.sum(returned.astype(jnp.float32), axis=0)

    doc_unit = unit_rows(pooled)
    cycle_size = lax.axis_size("blk")
    position = lax.axis_index("blk")
    arrived = jnp.stack(
        [doc_unit]
        + [
            lax.ppermute(doc_unit, "blk", [(i, (i + shift) % cycle_size) for i in range(cycle_size)])
            for shift in range(1, cycle_size)
        ]
    )
    arrival_of = (position - jnp.arange(cycle_size, dtype=jnp.int32)) % cycle_size
    doc_piece = arrived[arrival_of].reshape(cycle_size * doc_unit.shape[0], emb_width)
    piece_rows = doc_piece.shape[0]
    hits = (positives[:, None] == jnp.arange(piece_rows, dtype=jnp.int32)[None, :]).astype(
        jnp.bfloat16
    )
    loss_col, weights, totals, grad_part = scores(queries, doc_piece, hits)
    grad_docs = line_reduce_scatter(
        grad_part.reshape(cycle_size, doc_unit.shape[0], emb_width), "blk"
    )
    grad_queries = query_grads(weights, totals, hits, doc_piece)
    loss_rows = loss_col.reshape(loss_col.shape[0])
    return (loss_rows, grad_queries, grad_docs)


def solution(mesh):
    placed = (
        P(("dp", "blk"), None),
        P(("dp", "blk")),
        P(("dp", "blk")),
        P(("dp", "blk")),
        P("dp", None, None),
        P(),
        P(("dp", "blk"), None),
        P(("dp", "blk")),
    )
    return jax.shard_map(
        on_device,
        mesh=mesh,
        in_specs=placed,
        out_specs=(P(("dp", "blk")), P(("dp", "blk"), None), P(("dp", "blk"), None)),
        check_vma=False,
    )
```

```python
import jax
import jax.numpy as jnp
from jax import lax
from jax.experimental import pallas as pl
from jax.experimental.pallas import tpu as pltpu
from jax.sharding import PartitionSpec as P

SESS_DEV = 16


logit_scale = 20.0
epsilon = 1e-06


def unit_rows(values):
    widened = values.astype(jnp.float32)
    return (
        widened * lax.rsqrt(jnp.sum(widened * widened, axis=-1, keepdims=True) + epsilon)
    ).astype(jnp.bfloat16)


def contract_rows(left_side, right_side):
    return lax.dot_general(
        left_side, right_side, (((1,), (1,)), ((), ())), preferred_element_type=jnp.float32
    )


def contract_first(left_side, right_side):
    return lax.dot_general(
        left_side, right_side, (((0,), (0,)), ((), ())), preferred_element_type=jnp.float32
    )


def score_kernel(q_ref, d_ref, hit_ref, loss_ref, wb_ref, tot_ref, gd_ref):
    @pl.when(pl.program_id(0) == 0)
    def _():
        gd_ref[...] = jnp.zeros_like(gd_ref)

    query_unit = q_ref[...]
    logits = logit_scale * contract_rows(query_unit, d_ref[...])
    weights = jnp.exp(logits)
    totals = jnp.sum(weights, axis=1, keepdims=True)
    hits = hit_ref[...].astype(jnp.float32)
    chosen_logit = jnp.sum(hits * logits, axis=1, keepdims=True)
    loss_ref[...] = jnp.log(totals) - chosen_logit
    wb_ref[...] = weights.astype(jnp.bfloat16)
    tot_ref[...] = totals
    coefficient_t = (weights / totals - hits).T.astype(jnp.bfloat16)
    gd_ref[...] += logit_scale * jnp.dot(
        coefficient_t, query_unit, preferred_element_type=jnp.float32
    )


def query_grad_kernel(wb_ref, tot_ref, hit_ref, d_ref, gq_ref):
    docs = d_ref[...]
    numerator = jnp.dot(wb_ref[...], docs, preferred_element_type=jnp.float32)
    chosen_doc = jnp.dot(hit_ref[...], docs, preferred_element_type=jnp.float32)
    gq_ref[...] = (logit_scale * (numerator / tot_ref[...] - chosen_doc)).astype(jnp.bfloat16)


def scores(queries, doc_piece, hits, tile=128):
    rows, width = queries.shape
    docs = doc_piece.shape[0]
    return pl.pallas_call(
        score_kernel,
        grid=(rows // tile,),
        in_specs=[
            pl.BlockSpec((tile, width), lambda i: (i, 0)),
            pl.BlockSpec((docs, width), lambda i: (0, 0)),
            pl.BlockSpec((tile, docs), lambda i: (i, 0)),
        ],
        out_specs=[
            pl.BlockSpec((tile, 1), lambda i: (i, 0)),
            pl.BlockSpec((tile, docs), lambda i: (i, 0)),
            pl.BlockSpec((tile, 1), lambda i: (i, 0)),
            pl.BlockSpec((docs, width), lambda i: (0, 0)),
        ],
        out_shape=[
            jax.ShapeDtypeStruct((rows, 1), jnp.float32),
            jax.ShapeDtypeStruct((rows, docs), jnp.bfloat16),
            jax.ShapeDtypeStruct((rows, 1), jnp.float32),
            jax.ShapeDtypeStruct((docs, width), jnp.float32),
        ],
        compiler_params=pltpu.CompilerParams(dimension_semantics=("arbitrary",)),
        cost_estimate=pl.CostEstimate(
            flops=4 * rows * docs * width, transcendentals=rows * docs, bytes_accessed=2 * rows * width
        ),
    )(queries, doc_piece, hits)


def query_grads(weights, totals, hits, doc_piece, tile=128):
    rows, docs = weights.shape
    width = doc_piece.shape[1]
    return pl.pallas_call(
        query_grad_kernel,
        grid=(rows // tile,),
        in_specs=[
            pl.BlockSpec((tile, docs), lambda i: (i, 0)),
            pl.BlockSpec((tile, 1), lambda i: (i, 0)),
            pl.BlockSpec((tile, docs), lambda i: (i, 0)),
            pl.BlockSpec((docs, width), lambda i: (0, 0)),
        ],
        out_specs=pl.BlockSpec((tile, width), lambda i: (i, 0)),
        out_shape=jax.ShapeDtypeStruct((rows, width), jnp.bfloat16),
        compiler_params=pltpu.CompilerParams(dimension_semantics=("arbitrary",)),
        cost_estimate=pl.CostEstimate(
            flops=4 * rows * docs * width, transcendentals=0, bytes_accessed=2 * rows * width
        ),
    )(weights, totals, hits, doc_piece)


def on_device(
    spans, span_counts, session_ids, destinations, expert_weight, norm_gain, queries, positives
):
    rows_dev = spans.shape[0]
    hidden_width = spans.shape[1]
    groups = lax.axis_size("dp")
    capacity = (rows_dev - 3 * SESS_DEV) // groups
    received = rows_dev // 4
    cycle = rows_dev // groups
    count = span_counts[0]

    lane_of = (jnp.arange(groups, dtype=jnp.int32) - destinations[0]) % groups
    by_lane = spans.reshape(cycle, groups, hidden_width)
    send_rows = jnp.swapaxes(jnp.take(by_lane, lane_of, axis=1), 0, 1)[:, :capacity]
    row_of = lane_of[:, None] + groups * jnp.arange(capacity, dtype=jnp.int32)[None, :]
    ids_by_lane = session_ids.reshape(cycle, groups)
    send_ids = jnp.where(
        row_of < count, jnp.swapaxes(jnp.take(ids_by_lane, lane_of, axis=1), 0, 1)[:, :capacity], -1
    )
    got_rows = lax.all_to_all(send_rows, "dp", split_axis=0, concat_axis=0, tiled=True)
    got_ids = lax.all_to_all(send_ids, "dp", split_axis=0, concat_axis=0, tiled=True)

    got_counts = jnp.sum((got_ids >= 0).astype(jnp.int32), axis=1)
    starts = jnp.cumsum(got_counts) - got_counts
    packed_index = jnp.arange(received, dtype=jnp.int32)
    source_of = (
        jnp.sum((starts[None, :] <= packed_index[:, None]).astype(jnp.int32), axis=1) - 1
    )
    slot_of = source_of * capacity + packed_index - starts[source_of]
    packed_live = packed_index < jnp.sum(got_counts)
    slot_of = jnp.where(packed_live, slot_of, 0)
    packed = got_rows.reshape(groups * capacity, hidden_width)[slot_of]
    packed_key = jnp.where(
        packed_live, source_of * SESS_DEV + got_ids.reshape(groups * capacity)[slot_of], -1
    )

    widened = packed.astype(jnp.float32)
    normed = (
        widened
        * lax.rsqrt(jnp.mean(widened * widened, axis=-1, keepdims=True) + epsilon)
        * norm_gain
    ).astype(jnp.bfloat16)
    embedded = jax.nn.gelu(
        jnp.dot(normed, expert_weight[0], preferred_element_type=jnp.float32), approximate=True
    ).astype(jnp.bfloat16)
    emb_width = embedded.shape[1]
    selector = (
        jnp.arange(groups * SESS_DEV, dtype=jnp.int32)[:, None] == packed_key[None, :]
    ).astype(jnp.bfloat16)
    partial = jnp.dot(selector, embedded, preferred_element_type=jnp.float32)
    partial = partial.astype(jnp.bfloat16).reshape(groups, SESS_DEV, emb_width)
    returned = lax.all_to_all(partial, "dp", split_axis=0, concat_axis=0, tiled=True)
    pooled = jnp.sum(returned.astype(jnp.float32), axis=0)

    doc_unit = unit_rows(pooled)
    query_unit = unit_rows(queries)
    cycle_size = lax.axis_size("blk")
    position = lax.axis_index("blk")
    arrived = jnp.stack(
        [doc_unit]
        + [
            lax.ppermute(doc_unit, "blk", [(i, (i + shift) % cycle_size) for i in range(cycle_size)])
            for shift in range(1, cycle_size)
        ]
    )
    arrival_of = (position - jnp.arange(cycle_size, dtype=jnp.int32)) % cycle_size
    doc_piece = arrived[arrival_of].reshape(cycle_size * doc_unit.shape[0], emb_width)
    piece_rows = doc_piece.shape[0]
    hits = (positives[:, None] == jnp.arange(piece_rows, dtype=jnp.int32)[None, :]).astype(
        jnp.bfloat16
    )
    loss_col, weights, totals, grad_part = scores(query_unit, doc_piece, hits)
    grad_docs = lax.psum_scatter(grad_part, "blk", scatter_dimension=0, tiled=True)
    grad_queries = query_grads(weights, totals, hits, doc_piece)
    loss_rows = loss_col.reshape(loss_col.shape[0])
    return (loss_rows, grad_queries, grad_docs)


def solution(mesh):
    placed = (
        P(("dp", "blk"), None),
        P(("dp", "blk")),
        P(("dp", "blk")),
        P(("dp", "blk")),
        P("dp", None, None),
        P(),
        P(("dp", "blk"), None),
        P(("dp", "blk")),
    )
    return jax.shard_map(
        on_device,
        mesh=mesh,
        in_specs=placed,
        out_specs=(P(("dp", "blk")), P(("dp", "blk"), None), P(("dp", "blk"), None)),
        check_vma=False,
    )
```

```python
import jax
import jax.numpy as jnp
from jax import lax
from jax.experimental import pallas as pl
from jax.experimental.pallas import tpu as pltpu
from jax.sharding import PartitionSpec as P

SESS_DEV = 16


logit_scale = 20.0
epsilon = 1e-06


def unit_rows(values):
    widened = values.astype(jnp.float32)
    return (
        widened * lax.rsqrt(jnp.sum(widened * widened, axis=-1, keepdims=True) + epsilon)
    ).astype(jnp.bfloat16)


def contract_rows(left_side, right_side):
    return lax.dot_general(
        left_side, right_side, (((1,), (1,)), ((), ())), preferred_element_type=jnp.float32
    )


def contract_first(left_side, right_side):
    return lax.dot_general(
        left_side, right_side, (((0,), (0,)), ((), ())), preferred_element_type=jnp.float32
    )


def score_kernel(q_ref, d_ref, hit_ref, loss_ref, wb_ref, tot_ref, gd_ref):
    @pl.when(pl.program_id(0) == 0)
    def _():
        gd_ref[...] = jnp.zeros_like(gd_ref)

    query_unit = q_ref[...]
    logits = logit_scale * contract_rows(query_unit, d_ref[...])
    weights = jnp.exp(logits)
    totals = jnp.sum(weights, axis=1, keepdims=True)
    hits = hit_ref[...].astype(jnp.float32)
    chosen_logit = jnp.sum(hits * logits, axis=1, keepdims=True)
    loss_ref[...] = jnp.log(totals) - chosen_logit
    wb_ref[...] = weights.astype(jnp.bfloat16)
    tot_ref[...] = totals
    coefficient_t = (weights / totals - hits).T.astype(jnp.bfloat16)
    gd_ref[...] += logit_scale * jnp.dot(
        coefficient_t, query_unit, preferred_element_type=jnp.float32
    )


def query_grad_kernel(wb_ref, tot_ref, hit_ref, d_ref, gq_ref):
    docs = d_ref[...]
    numerator = jnp.dot(wb_ref[...], docs, preferred_element_type=jnp.float32)
    chosen_doc = jnp.dot(hit_ref[...], docs, preferred_element_type=jnp.float32)
    gq_ref[...] = (logit_scale * (numerator / tot_ref[...] - chosen_doc)).astype(jnp.bfloat16)


def scores(queries, doc_piece, hits, tile=128):
    rows, width = queries.shape
    docs = doc_piece.shape[0]
    return pl.pallas_call(
        score_kernel,
        grid=(rows // tile,),
        in_specs=[
            pl.BlockSpec((tile, width), lambda i: (i, 0)),
            pl.BlockSpec((docs, width), lambda i: (0, 0)),
            pl.BlockSpec((tile, docs), lambda i: (i, 0)),
        ],
        out_specs=[
            pl.BlockSpec((tile, 1), lambda i: (i, 0)),
            pl.BlockSpec((tile, docs), lambda i: (i, 0)),
            pl.BlockSpec((tile, 1), lambda i: (i, 0)),
            pl.BlockSpec((docs, width), lambda i: (0, 0)),
        ],
        out_shape=[
            jax.ShapeDtypeStruct((rows, 1), jnp.float32),
            jax.ShapeDtypeStruct((rows, docs), jnp.bfloat16),
            jax.ShapeDtypeStruct((rows, 1), jnp.float32),
            jax.ShapeDtypeStruct((docs, width), jnp.float32),
        ],
        compiler_params=pltpu.CompilerParams(dimension_semantics=("arbitrary",)),
        cost_estimate=pl.CostEstimate(
            flops=4 * rows * docs * width, transcendentals=rows * docs, bytes_accessed=2 * rows * width
        ),
    )(queries, doc_piece, hits)


def query_grads(weights, totals, hits, doc_piece, tile=128):
    rows, docs = weights.shape
    width = doc_piece.shape[1]
    return pl.pallas_call(
        query_grad_kernel,
        grid=(rows // tile,),
        in_specs=[
            pl.BlockSpec((tile, docs), lambda i: (i, 0)),
            pl.BlockSpec((tile, 1), lambda i: (i, 0)),
            pl.BlockSpec((tile, docs), lambda i: (i, 0)),
            pl.BlockSpec((docs, width), lambda i: (0, 0)),
        ],
        out_specs=pl.BlockSpec((tile, width), lambda i: (i, 0)),
        out_shape=jax.ShapeDtypeStruct((rows, width), jnp.bfloat16),
        compiler_params=pltpu.CompilerParams(dimension_semantics=("arbitrary",)),
        cost_estimate=pl.CostEstimate(
            flops=4 * rows * docs * width, transcendentals=0, bytes_accessed=2 * rows * width
        ),
    )(weights, totals, hits, doc_piece)


def on_device(
    spans, span_counts, session_ids, destinations, expert_weight, norm_gain, queries, positives
):
    rows_dev = spans.shape[0]
    hidden_width = spans.shape[1]
    groups = lax.axis_size("dp")
    capacity = (rows_dev - 3 * SESS_DEV) // groups
    received = rows_dev // 4
    count = span_counts[0]

    lane_of = (jnp.arange(groups, dtype=jnp.int32) - destinations[0]) % groups
    row_of = lane_of[:, None] + groups * jnp.arange(capacity, dtype=jnp.int32)[None, :]
    row_of = jnp.where(row_of < count, row_of, -1).reshape(groups * capacity)
    picker = (row_of[:, None] == jnp.arange(rows_dev, dtype=jnp.int32)[None, :]).astype(jnp.bfloat16)
    send_rows = (
        jnp.dot(picker, spans, preferred_element_type=jnp.float32)
        .astype(jnp.bfloat16)
        .reshape(groups, capacity, hidden_width)
    )
    send_ids = jnp.where(row_of >= 0, session_ids[jnp.maximum(row_of, 0)], -1).reshape(
        groups, capacity
    )
    got_rows = lax.all_to_all(send_rows, "dp", split_axis=0, concat_axis=0, tiled=True)
    query_unit = unit_rows(queries)
    got_rows, query_unit = lax.optimization_barrier((got_rows, query_unit))
    got_ids = lax.all_to_all(send_ids, "dp", split_axis=0, concat_axis=0, tiled=True)

    got_counts = jnp.sum((got_ids >= 0).astype(jnp.int32), axis=1)
    starts = jnp.cumsum(got_counts) - got_counts
    packed_index = jnp.arange(received, dtype=jnp.int32)
    source_of = (
        jnp.sum((starts[None, :] <= packed_index[:, None]).astype(jnp.int32), axis=1) - 1
    )
    slot_of = source_of * capacity + packed_index - starts[source_of]
    packed_live = packed_index < jnp.sum(got_counts)
    slot_of = jnp.where(packed_live, slot_of, 0)
    packed = got_rows.reshape(groups * capacity, hidden_width)[slot_of]
    packed_key = jnp.where(
        packed_live, source_of * SESS_DEV + got_ids.reshape(groups * capacity)[slot_of], -1
    )

    widened = packed.astype(jnp.float32)
    normed = (
        widened
        * lax.rsqrt(jnp.mean(widened * widened, axis=-1, keepdims=True) + epsilon)
        * norm_gain
    ).astype(jnp.bfloat16)
    embedded = jax.nn.gelu(
        jnp.dot(normed, expert_weight[0], preferred_element_type=jnp.float32), approximate=True
    ).astype(jnp.bfloat16)
    emb_width = embedded.shape[1]
    selector = (
        jnp.arange(groups * SESS_DEV, dtype=jnp.int32)[:, None] == packed_key[None, :]
    ).astype(jnp.bfloat16)
    partial = jnp.dot(selector, embedded, preferred_element_type=jnp.float32)
    partial = partial.astype(jnp.bfloat16).reshape(groups, SESS_DEV, emb_width)
    returned = lax.all_to_all(partial, "dp", split_axis=0, concat_axis=0, tiled=True)
    pooled = jnp.sum(returned.astype(jnp.float32), axis=0)

    doc_unit = unit_rows(pooled)
    cycle_size = lax.axis_size("blk")
    position = lax.axis_index("blk")
    arrived = jnp.stack(
        [doc_unit]
        + [
            lax.ppermute(doc_unit, "blk", [(i, (i + shift) % cycle_size) for i in range(cycle_size)])
            for shift in range(1, cycle_size)
        ]
    )
    arrival_of = (position - jnp.arange(cycle_size, dtype=jnp.int32)) % cycle_size
    doc_piece = arrived[arrival_of].reshape(cycle_size * doc_unit.shape[0], emb_width)
    piece_rows = doc_piece.shape[0]
    hits = (positives[:, None] == jnp.arange(piece_rows, dtype=jnp.int32)[None, :]).astype(
        jnp.bfloat16
    )
    loss_col, weights, totals, grad_part = scores(query_unit, doc_piece, hits)
    grad_docs = lax.psum_scatter(grad_part, "blk", scatter_dimension=0, tiled=True)
    grad_queries = query_grads(weights, totals, hits, doc_piece)
    loss_rows = loss_col.reshape(loss_col.shape[0])
    return (loss_rows, grad_queries, grad_docs)


def solution(mesh):
    placed = (
        P(("dp", "blk"), None),
        P(("dp", "blk")),
        P(("dp", "blk")),
        P(("dp", "blk")),
        P("dp", None, None),
        P(),
        P(("dp", "blk"), None),
        P(("dp", "blk")),
    )
    return jax.shard_map(
        on_device,
        mesh=mesh,
        in_specs=placed,
        out_specs=(P(("dp", "blk")), P(("dp", "blk"), None), P(("dp", "blk"), None)),
        check_vma=False,
    )
```

```python
import jax
import jax.numpy as jnp
from jax import lax
from jax.experimental import pallas as pl
from jax.experimental.pallas import tpu as pltpu
from jax.sharding import PartitionSpec as P

SESS_DEV = 16


logit_scale = 20.0
epsilon = 1e-06


def unit_rows(values):
    widened = values.astype(jnp.float32)
    return (
        widened * lax.rsqrt(jnp.sum(widened * widened, axis=-1, keepdims=True) + epsilon)
    ).astype(jnp.bfloat16)


def contract_rows(left_side, right_side):
    return lax.dot_general(
        left_side, right_side, (((1,), (1,)), ((), ())), preferred_element_type=jnp.float32
    )


def contract_first(left_side, right_side):
    return lax.dot_general(
        left_side, right_side, (((0,), (0,)), ((), ())), preferred_element_type=jnp.float32
    )


def score_kernel(q_ref, d_ref, hit_ref, loss_ref, wb_ref, tot_ref, gd_ref):
    @pl.when(pl.program_id(0) == 0)
    def _():
        gd_ref[...] = jnp.zeros_like(gd_ref)

    widened = q_ref[...].astype(jnp.float32)
    query_unit = (
        widened * lax.rsqrt(jnp.sum(widened * widened, axis=-1, keepdims=True) + epsilon)
    ).astype(jnp.bfloat16)
    logits = logit_scale * contract_rows(query_unit, d_ref[...])
    weights = jnp.exp(logits)
    totals = jnp.sum(weights, axis=1, keepdims=True)
    hits = hit_ref[...].astype(jnp.float32)
    chosen_logit = jnp.sum(hits * logits, axis=1, keepdims=True)
    loss_ref[...] = jnp.log(totals) - chosen_logit
    wb_ref[...] = weights.astype(jnp.bfloat16)
    tot_ref[...] = totals
    coefficient_t = (weights / totals - hits).T.astype(jnp.bfloat16)
    gd_ref[...] += logit_scale * jnp.dot(
        coefficient_t, query_unit, preferred_element_type=jnp.float32
    )


def query_grad_kernel(wb_ref, tot_ref, hit_ref, d_ref, gq_ref):
    docs = d_ref[...]
    numerator = jnp.dot(wb_ref[...], docs, preferred_element_type=jnp.float32)
    chosen_doc = jnp.dot(hit_ref[...], docs, preferred_element_type=jnp.float32)
    gq_ref[...] = (logit_scale * (numerator / tot_ref[...] - chosen_doc)).astype(jnp.bfloat16)


def scores(queries, doc_piece, hits, tile=128):
    rows, width = queries.shape
    docs = doc_piece.shape[0]
    return pl.pallas_call(
        score_kernel,
        grid=(rows // tile,),
        in_specs=[
            pl.BlockSpec((tile, width), lambda i: (i, 0)),
            pl.BlockSpec((docs, width), lambda i: (0, 0)),
            pl.BlockSpec((tile, docs), lambda i: (i, 0)),
        ],
        out_specs=[
            pl.BlockSpec((tile, 1), lambda i: (i, 0)),
            pl.BlockSpec((tile, docs), lambda i: (i, 0)),
            pl.BlockSpec((tile, 1), lambda i: (i, 0)),
            pl.BlockSpec((docs, width), lambda i: (0, 0)),
        ],
        out_shape=[
            jax.ShapeDtypeStruct((rows, 1), jnp.float32),
            jax.ShapeDtypeStruct((rows, docs), jnp.bfloat16),
            jax.ShapeDtypeStruct((rows, 1), jnp.float32),
            jax.ShapeDtypeStruct((docs, width), jnp.float32),
        ],
        compiler_params=pltpu.CompilerParams(dimension_semantics=("arbitrary",)),
        cost_estimate=pl.CostEstimate(
            flops=4 * rows * docs * width, transcendentals=rows * docs, bytes_accessed=2 * rows * width
        ),
    )(queries, doc_piece, hits)


def query_grads(weights, totals, hits, doc_piece, tile=128):
    rows, docs = weights.shape
    width = doc_piece.shape[1]
    return pl.pallas_call(
        query_grad_kernel,
        grid=(rows // tile,),
        in_specs=[
            pl.BlockSpec((tile, docs), lambda i: (i, 0)),
            pl.BlockSpec((tile, 1), lambda i: (i, 0)),
            pl.BlockSpec((tile, docs), lambda i: (i, 0)),
            pl.BlockSpec((docs, width), lambda i: (0, 0)),
        ],
        out_specs=pl.BlockSpec((tile, width), lambda i: (i, 0)),
        out_shape=jax.ShapeDtypeStruct((rows, width), jnp.bfloat16),
        compiler_params=pltpu.CompilerParams(dimension_semantics=("arbitrary",)),
        cost_estimate=pl.CostEstimate(
            flops=4 * rows * docs * width, transcendentals=0, bytes_accessed=2 * rows * width
        ),
    )(weights, totals, hits, doc_piece)


def on_device(
    spans, span_counts, session_ids, destinations, expert_weight, norm_gain, queries, positives
):
    rows_dev = spans.shape[0]
    hidden_width = spans.shape[1]
    groups = lax.axis_size("dp")
    capacity = (rows_dev - 3 * SESS_DEV) // groups
    received = rows_dev // 4
    cycle = rows_dev // groups
    count = span_counts[0]

    lane_of = (jnp.arange(groups, dtype=jnp.int32) - destinations[0]) % groups
    by_lane = spans.reshape(cycle, groups, hidden_width)
    send_rows = jnp.swapaxes(jnp.take(by_lane, lane_of, axis=1), 0, 1)[:, :capacity]
    row_of = lane_of[:, None] + groups * jnp.arange(capacity, dtype=jnp.int32)[None, :]
    ids_by_lane = session_ids.reshape(cycle, groups)
    send_ids = jnp.where(
        row_of < count, jnp.swapaxes(jnp.take(ids_by_lane, lane_of, axis=1), 0, 1)[:, :capacity], -1
    )
    got_rows = lax.all_to_all(send_rows, "dp", split_axis=0, concat_axis=0, tiled=True)
    got_ids = lax.all_to_all(send_ids, "dp", split_axis=0, concat_axis=0, tiled=True)

    got_counts = jnp.sum((got_ids >= 0).astype(jnp.int32), axis=1)
    starts = jnp.cumsum(got_counts) - got_counts
    packed_index = jnp.arange(received, dtype=jnp.int32)
    source_of = (
        jnp.sum((starts[None, :] <= packed_index[:, None]).astype(jnp.int32), axis=1) - 1
    )
    slot_of = source_of * capacity + packed_index - starts[source_of]
    packed_live = packed_index < jnp.sum(got_counts)
    slot_of = jnp.where(packed_live, slot_of, 0)
    packed = got_rows.reshape(groups * capacity, hidden_width)[slot_of]
    packed_key = jnp.where(
        packed_live, source_of * SESS_DEV + got_ids.reshape(groups * capacity)[slot_of], -1
    )

    widened = packed.astype(jnp.float32)
    normed = (
        widened
        * lax.rsqrt(jnp.mean(widened * widened, axis=-1, keepdims=True) + epsilon)
        * norm_gain
    ).astype(jnp.bfloat16)
    embedded = jax.nn.gelu(
        jnp.dot(normed, expert_weight[0], preferred_element_type=jnp.float32), approximate=True
    ).astype(jnp.bfloat16)
    emb_width = embedded.shape[1]
    selector = (
        jnp.arange(groups * SESS_DEV, dtype=jnp.int32)[:, None] == packed_key[None, :]
    ).astype(jnp.bfloat16)
    partial = jnp.dot(selector, embedded, preferred_element_type=jnp.float32)
    partial = partial.astype(jnp.bfloat16).reshape(groups, SESS_DEV, emb_width)
    returned = lax.all_to_all(partial, "dp", split_axis=0, concat_axis=0, tiled=True)
    pooled = jnp.sum(returned.astype(jnp.float32), axis=0)

    doc_unit = unit_rows(pooled)
    cycle_size = lax.axis_size("blk")
    position = lax.axis_index("blk")
    arrived = jnp.stack(
        [doc_unit]
        + [
            lax.ppermute(doc_unit, "blk", [(i, (i + shift) % cycle_size) for i in range(cycle_size)])
            for shift in range(1, cycle_size)
        ]
    )
    arrival_of = (position - jnp.arange(cycle_size, dtype=jnp.int32)) % cycle_size
    doc_piece = arrived[arrival_of].reshape(cycle_size * doc_unit.shape[0], emb_width)
    piece_rows = doc_piece.shape[0]
    hits = (positives[:, None] == jnp.arange(piece_rows, dtype=jnp.int32)[None, :]).astype(
        jnp.bfloat16
    )
    loss_col, weights, totals, grad_part = scores(queries, doc_piece, hits)
    grad_terms = lax.all_to_all(
        grad_part.astype(jnp.bfloat16).reshape(cycle_size, doc_unit.shape[0], emb_width),
        "blk",
        split_axis=0,
        concat_axis=0,
        tiled=True,
    )
    grad_docs = jnp.sum(grad_terms.astype(jnp.float32), axis=0)
    grad_queries = query_grads(weights, totals, hits, doc_piece)
    loss_rows = loss_col.reshape(loss_col.shape[0])
    return (loss_rows, grad_queries, grad_docs)


def solution(mesh):
    placed = (
        P(("dp", "blk"), None),
        P(("dp", "blk")),
        P(("dp", "blk")),
        P(("dp", "blk")),
        P("dp", None, None),
        P(),
        P(("dp", "blk"), None),
        P(("dp", "blk")),
    )
    return jax.shard_map(
        on_device,
        mesh=mesh,
        in_specs=placed,
        out_specs=(P(("dp", "blk")), P(("dp", "blk"), None), P(("dp", "blk"), None)),
        check_vma=False,
    )
```

```python
import jax
import jax.numpy as jnp
from jax import lax
from jax.experimental import pallas as pl
from jax.experimental.pallas import tpu as pltpu
from jax.sharding import PartitionSpec as P

SESS_DEV = 16


logit_scale = 20.0
epsilon = 1e-06


def unit_rows(values):
    widened = values.astype(jnp.float32)
    return (
        widened * lax.rsqrt(jnp.sum(widened * widened, axis=-1, keepdims=True) + epsilon)
    ).astype(jnp.bfloat16)


def contract_rows(left_side, right_side):
    return lax.dot_general(
        left_side, right_side, (((1,), (1,)), ((), ())), preferred_element_type=jnp.float32
    )


def contract_first(left_side, right_side):
    return lax.dot_general(
        left_side, right_side, (((0,), (0,)), ((), ())), preferred_element_type=jnp.float32
    )


def score_kernel(q_ref, d_ref, hit_ref, loss_ref, wb_ref, tot_ref, gd_ref, acc_ref):
    @pl.when(pl.program_id(0) == 0)
    def _():
        acc_ref[...] = jnp.zeros_like(acc_ref)

    widened = q_ref[...].astype(jnp.float32)
    query_unit = (
        widened * lax.rsqrt(jnp.sum(widened * widened, axis=-1, keepdims=True) + epsilon)
    ).astype(jnp.bfloat16)
    logits = logit_scale * contract_rows(query_unit, d_ref[...])
    weights = jnp.exp(logits)
    totals = jnp.sum(weights, axis=1, keepdims=True)
    hits = hit_ref[...].astype(jnp.float32)
    chosen_logit = jnp.sum(hits * logits, axis=1, keepdims=True)
    loss_ref[...] = jnp.log(totals) - chosen_logit
    wb_ref[...] = weights.astype(jnp.bfloat16)
    tot_ref[...] = totals
    coefficient_t = (weights / totals - hits).T.astype(jnp.bfloat16)
    acc_ref[...] += logit_scale * jnp.dot(
        coefficient_t, query_unit, preferred_element_type=jnp.float32
    )

    @pl.when(pl.program_id(0) == pl.num_programs(0) - 1)
    def _():
        gd_ref[...] = acc_ref[...].astype(jnp.bfloat16)


def query_grad_kernel(wb_ref, tot_ref, hit_ref, d_ref, gq_ref):
    docs = d_ref[...]
    numerator = jnp.dot(wb_ref[...], docs, preferred_element_type=jnp.float32)
    chosen_doc = jnp.dot(hit_ref[...], docs, preferred_element_type=jnp.float32)
    gq_ref[...] = (logit_scale * (numerator / tot_ref[...] - chosen_doc)).astype(jnp.bfloat16)


def scores(queries, doc_piece, hits, tile=128):
    rows, width = queries.shape
    docs = doc_piece.shape[0]
    return pl.pallas_call(
        score_kernel,
        grid=(rows // tile,),
        in_specs=[
            pl.BlockSpec((tile, width), lambda i: (i, 0)),
            pl.BlockSpec((docs, width), lambda i: (0, 0)),
            pl.BlockSpec((tile, docs), lambda i: (i, 0)),
        ],
        out_specs=[
            pl.BlockSpec((tile, 1), lambda i: (i, 0)),
            pl.BlockSpec((tile, docs), lambda i: (i, 0)),
            pl.BlockSpec((tile, 1), lambda i: (i, 0)),
            pl.BlockSpec((docs, width), lambda i: (0, 0)),
        ],
        out_shape=[
            jax.ShapeDtypeStruct((rows, 1), jnp.float32),
            jax.ShapeDtypeStruct((rows, docs), jnp.bfloat16),
            jax.ShapeDtypeStruct((rows, 1), jnp.float32),
            jax.ShapeDtypeStruct((docs, width), jnp.bfloat16),
        ],
        scratch_shapes=[pltpu.VMEM((docs, width), jnp.float32)],
        compiler_params=pltpu.CompilerParams(dimension_semantics=("arbitrary",)),
        cost_estimate=pl.CostEstimate(
            flops=4 * rows * docs * width, transcendentals=rows * docs, bytes_accessed=2 * rows * width
        ),
    )(queries, doc_piece, hits)


def query_grads(weights, totals, hits, doc_piece, tile=128):
    rows, docs = weights.shape
    width = doc_piece.shape[1]
    return pl.pallas_call(
        query_grad_kernel,
        grid=(rows // tile,),
        in_specs=[
            pl.BlockSpec((tile, docs), lambda i: (i, 0)),
            pl.BlockSpec((tile, 1), lambda i: (i, 0)),
            pl.BlockSpec((tile, docs), lambda i: (i, 0)),
            pl.BlockSpec((docs, width), lambda i: (0, 0)),
        ],
        out_specs=pl.BlockSpec((tile, width), lambda i: (i, 0)),
        out_shape=jax.ShapeDtypeStruct((rows, width), jnp.bfloat16),
        compiler_params=pltpu.CompilerParams(dimension_semantics=("arbitrary",)),
        cost_estimate=pl.CostEstimate(
            flops=4 * rows * docs * width, transcendentals=0, bytes_accessed=2 * rows * width
        ),
    )(weights, totals, hits, doc_piece)


def on_device(
    spans, span_counts, session_ids, destinations, expert_weight, norm_gain, queries, positives
):
    rows_dev = spans.shape[0]
    hidden_width = spans.shape[1]
    groups = lax.axis_size("dp")
    capacity = (rows_dev - 3 * SESS_DEV) // groups
    received = rows_dev // 4
    cycle = rows_dev // groups
    count = span_counts[0]

    lane_of = (jnp.arange(groups, dtype=jnp.int32) - destinations[0]) % groups
    by_lane = spans.reshape(cycle, groups, hidden_width)
    send_rows = jnp.swapaxes(jnp.take(by_lane, lane_of, axis=1, mode="clip"), 0, 1)[
        :, :capacity
    ]
    row_of = lane_of[:, None] + groups * jnp.arange(capacity, dtype=jnp.int32)[None, :]
    ids_by_lane = session_ids.reshape(cycle, groups)
    send_ids = jnp.where(
        row_of < count, jnp.swapaxes(jnp.take(ids_by_lane, lane_of, axis=1, mode="clip"), 0, 1)[:, :capacity], -1
    )
    got_rows = lax.all_to_all(send_rows, "dp", split_axis=0, concat_axis=0, tiled=True)
    got_ids = lax.all_to_all(send_ids, "dp", split_axis=0, concat_axis=0, tiled=True)

    got_counts = jnp.sum((got_ids >= 0).astype(jnp.int32), axis=1)
    starts = jnp.cumsum(got_counts) - got_counts
    packed_index = jnp.arange(received, dtype=jnp.int32)
    source_of = (
        jnp.sum((starts[None, :] <= packed_index[:, None]).astype(jnp.int32), axis=1) - 1
    )
    slot_of = source_of * capacity + packed_index - starts[source_of]
    packed_live = packed_index < jnp.sum(got_counts)
    slot_of = jnp.where(packed_live, slot_of, 0)
    packed = got_rows[source_of, jnp.where(packed_live, packed_index - starts[source_of], 0)]
    packed_key = jnp.where(
        packed_live, source_of * SESS_DEV + got_ids.reshape(groups * capacity)[slot_of], -1
    )

    widened = packed.astype(jnp.float32)
    normed = (
        widened
        * lax.rsqrt(jnp.mean(widened * widened, axis=-1, keepdims=True) + epsilon)
        * norm_gain
    ).astype(jnp.bfloat16)
    embedded = jax.nn.gelu(
        jnp.dot(normed, expert_weight[0], preferred_element_type=jnp.float32), approximate=True
    ).astype(jnp.bfloat16)
    emb_width = embedded.shape[1]
    selector = (
        jnp.arange(groups * SESS_DEV, dtype=jnp.int32)[:, None] == packed_key[None, :]
    ).astype(jnp.bfloat16)
    partial = jnp.dot(selector, embedded, preferred_element_type=jnp.float32)
    partial = partial.astype(jnp.bfloat16).reshape(groups, SESS_DEV, emb_width)
    returned = lax.all_to_all(partial, "dp", split_axis=0, concat_axis=0, tiled=True)
    pooled = jnp.sum(returned.astype(jnp.float32), axis=0)

    doc_unit = unit_rows(pooled)
    cycle_size = lax.axis_size("blk")
    position = lax.axis_index("blk")
    arrived = jnp.stack(
        [doc_unit]
        + [
            lax.ppermute(doc_unit, "blk", [(i, (i + shift) % cycle_size) for i in range(cycle_size)])
            for shift in range(1, cycle_size)
        ]
    )
    arrival_of = (position - jnp.arange(cycle_size, dtype=jnp.int32)) % cycle_size
    doc_piece = arrived[arrival_of].reshape(cycle_size * doc_unit.shape[0], emb_width)
    piece_rows = doc_piece.shape[0]
    hits = (positives[:, None] == jnp.arange(piece_rows, dtype=jnp.int32)[None, :]).astype(
        jnp.bfloat16
    )
    loss_col, weights, totals, grad_part = scores(queries, doc_piece, hits)
    grad_terms = lax.all_to_all(
        grad_part.reshape(cycle_size, doc_unit.shape[0], emb_width),
        "blk",
        split_axis=0,
        concat_axis=0,
        tiled=True,
    )
    grad_docs = jnp.sum(grad_terms.astype(jnp.float32), axis=0)
    grad_queries = query_grads(weights, totals, hits, doc_piece)
    loss_rows = loss_col.reshape(loss_col.shape[0])
    return (loss_rows, grad_queries, grad_docs)


def solution(mesh):
    placed = (
        P(("dp", "blk"), None),
        P(("dp", "blk")),
        P(("dp", "blk")),
        P(("dp", "blk")),
        P("dp", None, None),
        P(),
        P(("dp", "blk"), None),
        P(("dp", "blk")),
    )
    return jax.shard_map(
        on_device,
        mesh=mesh,
        in_specs=placed,
        out_specs=(P(("dp", "blk")), P(("dp", "blk"), None), P(("dp", "blk"), None)),
        check_vma=False,
    )
```

```python
import jax
import jax.numpy as jnp
from jax import lax
from jax.experimental import pallas as pl
from jax.experimental.pallas import tpu as pltpu
from jax.sharding import PartitionSpec as P

SESS_DEV = 16


logit_scale = 20.0
epsilon = 1e-06


def unit_rows(values):
    widened = values.astype(jnp.float32)
    return (
        widened * lax.rsqrt(jnp.sum(widened * widened, axis=-1, keepdims=True) + epsilon)
    ).astype(jnp.bfloat16)


def contract_rows(left_side, right_side):
    return lax.dot_general(
        left_side, right_side, (((1,), (1,)), ((), ())), preferred_element_type=jnp.float32
    )


def contract_first(left_side, right_side):
    return lax.dot_general(
        left_side, right_side, (((0,), (0,)), ((), ())), preferred_element_type=jnp.float32
    )


def score_kernel(q_ref, d_ref, hit_ref, loss_ref, wb_ref, tot_ref, gd_ref, acc_ref):
    @pl.when(pl.program_id(0) == 0)
    def _():
        acc_ref[...] = jnp.zeros_like(acc_ref)

    widened = q_ref[...].astype(jnp.float32)
    query_unit = (
        widened * lax.rsqrt(jnp.sum(widened * widened, axis=-1, keepdims=True) + epsilon)
    ).astype(jnp.bfloat16)
    logits = logit_scale * contract_rows(query_unit, d_ref[...])
    weights = jnp.exp(logits)
    totals = jnp.sum(weights, axis=1, keepdims=True)
    hits = hit_ref[...].astype(jnp.float32)
    chosen_logit = jnp.sum(hits * logits, axis=1, keepdims=True)
    loss_ref[...] = jnp.log(totals) - chosen_logit
    wb_ref[...] = weights.astype(jnp.bfloat16)
    tot_ref[...] = totals
    coefficient_t = (weights / totals - hits).T.astype(jnp.bfloat16)
    acc_ref[...] += logit_scale * jnp.dot(
        coefficient_t, query_unit, preferred_element_type=jnp.float32
    )

    @pl.when(pl.program_id(0) == pl.num_programs(0) - 1)
    def _():
        gd_ref[...] = acc_ref[...].astype(jnp.bfloat16)


def query_grad_kernel(wb_ref, tot_ref, hit_ref, d_ref, gq_ref):
    docs = d_ref[...]
    numerator = jnp.dot(wb_ref[...], docs, preferred_element_type=jnp.float32)
    chosen_doc = jnp.dot(hit_ref[...], docs, preferred_element_type=jnp.float32)
    gq_ref[...] = (logit_scale * (numerator / tot_ref[...] - chosen_doc)).astype(jnp.bfloat16)


def scores(queries, doc_piece, hits, tile=128):
    rows, width = queries.shape
    docs = doc_piece.shape[0]
    return pl.pallas_call(
        score_kernel,
        grid=(rows // tile,),
        in_specs=[
            pl.BlockSpec((tile, width), lambda i: (i, 0)),
            pl.BlockSpec((docs, width), lambda i: (0, 0)),
            pl.BlockSpec((tile, docs), lambda i: (i, 0)),
        ],
        out_specs=[
            pl.BlockSpec((tile, 1), lambda i: (i, 0)),
            pl.BlockSpec((tile, docs), lambda i: (i, 0)),
            pl.BlockSpec((tile, 1), lambda i: (i, 0)),
            pl.BlockSpec((docs, width), lambda i: (0, 0)),
        ],
        out_shape=[
            jax.ShapeDtypeStruct((rows, 1), jnp.float32),
            jax.ShapeDtypeStruct((rows, docs), jnp.bfloat16),
            jax.ShapeDtypeStruct((rows, 1), jnp.float32),
            jax.ShapeDtypeStruct((docs, width), jnp.bfloat16),
        ],
        scratch_shapes=[pltpu.VMEM((docs, width), jnp.float32)],
        compiler_params=pltpu.CompilerParams(dimension_semantics=("arbitrary",)),
        cost_estimate=pl.CostEstimate(
            flops=4 * rows * docs * width, transcendentals=rows * docs, bytes_accessed=2 * rows * width
        ),
    )(queries, doc_piece, hits)


def query_grads(weights, totals, hits, doc_piece, tile=128):
    rows, docs = weights.shape
    width = doc_piece.shape[1]
    return pl.pallas_call(
        query_grad_kernel,
        grid=(rows // tile,),
        in_specs=[
            pl.BlockSpec((tile, docs), lambda i: (i, 0)),
            pl.BlockSpec((tile, 1), lambda i: (i, 0)),
            pl.BlockSpec((tile, docs), lambda i: (i, 0)),
            pl.BlockSpec((docs, width), lambda i: (0, 0)),
        ],
        out_specs=pl.BlockSpec((tile, width), lambda i: (i, 0)),
        out_shape=jax.ShapeDtypeStruct((rows, width), jnp.bfloat16),
        compiler_params=pltpu.CompilerParams(dimension_semantics=("arbitrary",)),
        cost_estimate=pl.CostEstimate(
            flops=4 * rows * docs * width, transcendentals=0, bytes_accessed=2 * rows * width
        ),
    )(weights, totals, hits, doc_piece)


def on_device(
    spans, span_counts, session_ids, destinations, expert_weight, norm_gain, queries, positives
):
    rows_dev = spans.shape[0]
    hidden_width = spans.shape[1]
    groups = lax.axis_size("dp")
    capacity = (rows_dev - 3 * SESS_DEV) // groups
    received = rows_dev // 4
    cycle = rows_dev // groups
    count = span_counts[0]

    lane_of = (jnp.arange(groups, dtype=jnp.int32) - destinations[0]) % groups
    by_lane = spans.reshape(cycle, groups, hidden_width)
    send_rows = jnp.swapaxes(jnp.take(by_lane, lane_of, axis=1, mode="clip"), 0, 1)[
        :, :capacity
    ]
    row_of = lane_of[:, None] + groups * jnp.arange(capacity, dtype=jnp.int32)[None, :]
    ids_by_lane = session_ids.reshape(cycle, groups)
    send_ids = jnp.where(
        row_of < count, jnp.swapaxes(jnp.take(ids_by_lane, lane_of, axis=1, mode="clip"), 0, 1)[:, :capacity], -1
    )
    got_rows = lax.all_to_all(send_rows, "dp", split_axis=0, concat_axis=0, tiled=True)
    got_ids = lax.all_to_all(send_ids, "dp", split_axis=0, concat_axis=0, tiled=True)

    got_counts = jnp.sum((got_ids >= 0).astype(jnp.int32), axis=1)
    starts = jnp.cumsum(got_counts) - got_counts
    packed_index = jnp.arange(received, dtype=jnp.int32)
    source_of = (
        jnp.sum((starts[None, :] <= packed_index[:, None]).astype(jnp.int32), axis=1) - 1
    )
    slot_of = source_of * capacity + packed_index - starts[source_of]
    packed_live = packed_index < jnp.sum(got_counts)
    slot_of = jnp.where(packed_live, slot_of, 0)
    packed = got_rows.reshape(groups * capacity, hidden_width)[slot_of]
    packed_key = jnp.where(
        packed_live, source_of * SESS_DEV + got_ids.reshape(groups * capacity)[slot_of], -1
    )

    widened = packed.astype(jnp.float32)
    normed = (
        widened
        * lax.rsqrt(jnp.mean(widened * widened, axis=-1, keepdims=True) + epsilon)
        * norm_gain
    ).astype(jnp.bfloat16)
    embedded = jax.nn.gelu(
        jnp.dot(normed, expert_weight[0], preferred_element_type=jnp.float32), approximate=True
    ).astype(jnp.bfloat16)
    emb_width = embedded.shape[1]
    selector = (
        jnp.arange(groups * SESS_DEV, dtype=jnp.int32)[:, None] == packed_key[None, :]
    ).astype(jnp.bfloat16)
    partial = jnp.dot(selector, embedded, preferred_element_type=jnp.float32)
    partial = partial.astype(jnp.bfloat16).reshape(groups, SESS_DEV, emb_width)
    returned = lax.all_to_all(partial, "dp", split_axis=0, concat_axis=0, tiled=True)
    pooled = jnp.sum(returned.astype(jnp.float32), axis=0)

    doc_unit = unit_rows(pooled)
    cycle_size = lax.axis_size("blk")
    position = lax.axis_index("blk")
    arrived = jnp.stack(
        [doc_unit]
        + [
            lax.ppermute(doc_unit, "blk", [(i, (i + shift) % cycle_size) for i in range(cycle_size)])
            for shift in range(1, cycle_size)
        ]
    )
    arrival_of = (position - jnp.arange(cycle_size, dtype=jnp.int32)) % cycle_size
    doc_piece = arrived[arrival_of].reshape(cycle_size * doc_unit.shape[0], emb_width)
    piece_rows = doc_piece.shape[0]
    hits = (positives[:, None] == jnp.arange(piece_rows, dtype=jnp.int32)[None, :]).astype(
        jnp.bfloat16
    )
    loss_col, weights, totals, grad_part = scores(queries, doc_piece, hits)
    grad_terms = lax.all_to_all(
        grad_part.reshape(cycle_size, doc_unit.shape[0], emb_width),
        "blk",
        split_axis=0,
        concat_axis=0,
        tiled=True,
    )
    grad_docs = jnp.sum(grad_terms.astype(jnp.float32), axis=0)
    grad_queries = query_grads(weights, totals, hits, doc_piece)
    loss_rows = loss_col.reshape(loss_col.shape[0])
    return (loss_rows, grad_queries, grad_docs)


def solution(mesh):
    placed = (
        P(("dp", "blk"), None),
        P(("dp", "blk")),
        P(("dp", "blk")),
        P(("dp", "blk")),
        P("dp", None, None),
        P(),
        P(("dp", "blk"), None),
        P(("dp", "blk")),
    )
    return jax.shard_map(
        on_device,
        mesh=mesh,
        in_specs=placed,
        out_specs=(P(("dp", "blk")), P(("dp", "blk"), None), P(("dp", "blk"), None)),
        check_vma=False,
    )
```

```python
import jax
import jax.numpy as jnp
from jax import lax
from jax.experimental import pallas as pl
from jax.experimental.pallas import tpu as pltpu
from jax.sharding import PartitionSpec as P

SESS_DEV = 16


logit_scale = 20.0
epsilon = 1e-06


def unit_rows(values):
    widened = values.astype(jnp.float32)
    return (
        widened * lax.rsqrt(jnp.sum(widened * widened, axis=-1, keepdims=True) + epsilon)
    ).astype(jnp.bfloat16)


def contract_rows(left_side, right_side):
    return lax.dot_general(
        left_side, right_side, (((1,), (1,)), ((), ())), preferred_element_type=jnp.float32
    )


def contract_first(left_side, right_side):
    return lax.dot_general(
        left_side, right_side, (((0,), (0,)), ((), ())), preferred_element_type=jnp.float32
    )


def score_kernel(q_ref, d_ref, hit_ref, loss_ref, wb_ref, tot_ref, gd_ref, acc_ref):
    @pl.when(pl.program_id(0) == 0)
    def _():
        acc_ref[...] = jnp.zeros_like(acc_ref)

    widened = q_ref[...].astype(jnp.float32)
    query_unit = (
        widened * lax.rsqrt(jnp.sum(widened * widened, axis=-1, keepdims=True) + epsilon)
    ).astype(jnp.bfloat16)
    logits = logit_scale * contract_rows(query_unit, d_ref[...])
    weights = jnp.exp(logits)
    totals = jnp.sum(weights, axis=1, keepdims=True)
    hits = hit_ref[...].astype(jnp.float32)
    chosen_logit = jnp.sum(hits * logits, axis=1, keepdims=True)
    loss_ref[...] = jnp.log(totals) - chosen_logit
    wb_ref[...] = weights.astype(jnp.bfloat16)
    tot_ref[...] = totals
    coefficient_t = (weights / totals - hits).T.astype(jnp.bfloat16)
    acc_ref[...] += logit_scale * jnp.dot(
        coefficient_t, query_unit, preferred_element_type=jnp.float32
    )

    @pl.when(pl.program_id(0) == pl.num_programs(0) - 1)
    def _():
        gd_ref[...] = acc_ref[...].astype(jnp.bfloat16)


def query_grad_kernel(wb_ref, tot_ref, hit_ref, d_ref, gq_ref):
    docs = d_ref[...]
    numerator = jnp.dot(wb_ref[...], docs, preferred_element_type=jnp.float32)
    chosen_doc = jnp.dot(hit_ref[...], docs, preferred_element_type=jnp.float32)
    gq_ref[...] = (logit_scale * (numerator / tot_ref[...] - chosen_doc)).astype(jnp.bfloat16)


def scores(queries, doc_piece, hits, tile=128):
    rows, width = queries.shape
    docs = doc_piece.shape[0]
    return pl.pallas_call(
        score_kernel,
        grid=(rows // tile,),
        in_specs=[
            pl.BlockSpec((tile, width), lambda i: (i, 0)),
            pl.BlockSpec((docs, width), lambda i: (0, 0)),
            pl.BlockSpec((tile, docs), lambda i: (i, 0)),
        ],
        out_specs=[
            pl.BlockSpec((tile, 1), lambda i: (i, 0)),
            pl.BlockSpec((tile, docs), lambda i: (i, 0)),
            pl.BlockSpec((tile, 1), lambda i: (i, 0)),
            pl.BlockSpec((docs, width), lambda i: (0, 0)),
        ],
        out_shape=[
            jax.ShapeDtypeStruct((rows, 1), jnp.float32),
            jax.ShapeDtypeStruct((rows, docs), jnp.bfloat16),
            jax.ShapeDtypeStruct((rows, 1), jnp.float32),
            jax.ShapeDtypeStruct((docs, width), jnp.bfloat16),
        ],
        scratch_shapes=[pltpu.VMEM((docs, width), jnp.float32)],
        compiler_params=pltpu.CompilerParams(dimension_semantics=("arbitrary",)),
        cost_estimate=pl.CostEstimate(
            flops=4 * rows * docs * width, transcendentals=rows * docs, bytes_accessed=2 * rows * width
        ),
    )(queries, doc_piece, hits)


def query_grads(weights, totals, hits, doc_piece, tile=128):
    rows, docs = weights.shape
    width = doc_piece.shape[1]
    return pl.pallas_call(
        query_grad_kernel,
        grid=(rows // tile,),
        in_specs=[
            pl.BlockSpec((tile, docs), lambda i: (i, 0)),
            pl.BlockSpec((tile, 1), lambda i: (i, 0)),
            pl.BlockSpec((tile, docs), lambda i: (i, 0)),
            pl.BlockSpec((docs, width), lambda i: (0, 0)),
        ],
        out_specs=pl.BlockSpec((tile, width), lambda i: (i, 0)),
        out_shape=jax.ShapeDtypeStruct((rows, width), jnp.bfloat16),
        compiler_params=pltpu.CompilerParams(dimension_semantics=("arbitrary",)),
        cost_estimate=pl.CostEstimate(
            flops=4 * rows * docs * width, transcendentals=0, bytes_accessed=2 * rows * width
        ),
    )(weights, totals, hits, doc_piece)


def on_device(
    spans, span_counts, session_ids, destinations, expert_weight, norm_gain, queries, positives
):
    rows_dev = spans.shape[0]
    hidden_width = spans.shape[1]
    groups = lax.axis_size("dp")
    capacity = (rows_dev - 3 * SESS_DEV) // groups
    received = rows_dev // 4
    cycle = rows_dev // groups
    count = span_counts[0]

    lane_of = (jnp.arange(groups, dtype=jnp.int32) - destinations[0]) % groups
    by_lane = spans.reshape(cycle, groups, hidden_width)
    send_rows = jnp.swapaxes(jnp.take(by_lane, lane_of, axis=1, mode="clip"), 0, 1)[
        :, :capacity
    ]
    row_of = lane_of[:, None] + groups * jnp.arange(capacity, dtype=jnp.int32)[None, :]
    ids_by_lane = session_ids.reshape(cycle, groups)
    send_ids = jnp.where(
        row_of < count, jnp.swapaxes(jnp.take(ids_by_lane, lane_of, axis=1, mode="clip"), 0, 1)[:, :capacity], -1
    )
    got_rows = lax.all_to_all(send_rows, "dp", split_axis=0, concat_axis=0, tiled=True)
    got_ids = lax.all_to_all(send_ids, "dp", split_axis=0, concat_axis=0, tiled=True)

    got_counts = jnp.sum((got_ids >= 0).astype(jnp.int32), axis=1)
    starts = jnp.cumsum(got_counts) - got_counts
    packed_index = jnp.arange(received, dtype=jnp.int32)
    source_of = (
        jnp.sum((starts[None, :] <= packed_index[:, None]).astype(jnp.int32), axis=1) - 1
    )
    slot_of = source_of * capacity + packed_index - starts[source_of]
    packed_live = packed_index < jnp.sum(got_counts)
    slot_of = jnp.where(packed_live, slot_of, 0)
    packed = got_rows.reshape(groups * capacity, hidden_width)[slot_of]
    packed_key = jnp.where(
        packed_live, source_of * SESS_DEV + got_ids.reshape(groups * capacity)[slot_of], -1
    )

    widened = packed.astype(jnp.float32)
    normed = (
        widened
        * lax.rsqrt(jnp.mean(widened * widened, axis=-1, keepdims=True) + epsilon)
        * norm_gain
    ).astype(jnp.bfloat16)
    embedded = jax.nn.gelu(
        jnp.dot(normed, expert_weight[0], preferred_element_type=jnp.float32), approximate=True
    ).astype(jnp.bfloat16)
    emb_width = embedded.shape[1]
    selector = (
        jnp.arange(groups * SESS_DEV, dtype=jnp.int32)[:, None] == packed_key[None, :]
    ).astype(jnp.bfloat16)
    partial = jnp.dot(selector, embedded, preferred_element_type=jnp.float32)
    partial = partial.astype(jnp.bfloat16).reshape(groups, SESS_DEV, emb_width)
    returned = lax.all_to_all(partial, "dp", split_axis=0, concat_axis=0, tiled=True)
    pooled = jnp.sum(returned.astype(jnp.float32), axis=0)

    doc_unit = unit_rows(pooled)
    cycle_size = lax.axis_size("blk")
    doc_piece = lax.all_to_all(
        jnp.broadcast_to(doc_unit[None], (cycle_size,) + doc_unit.shape),
        "blk",
        split_axis=0,
        concat_axis=0,
        tiled=True,
    ).reshape(cycle_size * doc_unit.shape[0], emb_width)
    piece_rows = doc_piece.shape[0]
    hits = (positives[:, None] == jnp.arange(piece_rows, dtype=jnp.int32)[None, :]).astype(
        jnp.bfloat16
    )
    loss_col, weights, totals, grad_part = scores(queries, doc_piece, hits)
    grad_terms = lax.all_to_all(
        grad_part.reshape(cycle_size, doc_unit.shape[0], emb_width),
        "blk",
        split_axis=0,
        concat_axis=0,
        tiled=True,
    )
    grad_docs = jnp.sum(grad_terms.astype(jnp.float32), axis=0)
    grad_queries = query_grads(weights, totals, hits, doc_piece)
    loss_rows = loss_col.reshape(loss_col.shape[0])
    return (loss_rows, grad_queries, grad_docs)


def solution(mesh):
    placed = (
        P(("dp", "blk"), None),
        P(("dp", "blk")),
        P(("dp", "blk")),
        P(("dp", "blk")),
        P("dp", None, None),
        P(),
        P(("dp", "blk"), None),
        P(("dp", "blk")),
    )
    return jax.shard_map(
        on_device,
        mesh=mesh,
        in_specs=placed,
        out_specs=(P(("dp", "blk")), P(("dp", "blk"), None), P(("dp", "blk"), None)),
        check_vma=False,
    )
```

```python
import jax
import jax.numpy as jnp
from jax import lax
from jax.experimental import pallas as pl
from jax.experimental.pallas import tpu as pltpu
from jax.sharding import PartitionSpec as P

SESS_DEV = 16


logit_scale = 20.0
epsilon = 1e-06


def unit_rows(values):
    widened = values.astype(jnp.float32)
    return (
        widened * lax.rsqrt(jnp.sum(widened * widened, axis=-1, keepdims=True) + epsilon)
    ).astype(jnp.bfloat16)


def contract_rows(left_side, right_side):
    return lax.dot_general(
        left_side, right_side, (((1,), (1,)), ((), ())), preferred_element_type=jnp.float32
    )


def contract_first(left_side, right_side):
    return lax.dot_general(
        left_side, right_side, (((0,), (0,)), ((), ())), preferred_element_type=jnp.float32
    )


def score_kernel(q_ref, d_ref, hit_ref, loss_ref, wb_ref, tot_ref, gd_ref, acc_ref):
    @pl.when(pl.program_id(0) == 0)
    def _():
        acc_ref[...] = jnp.zeros_like(acc_ref)

    widened = q_ref[...].astype(jnp.float32)
    query_unit = (
        widened * lax.rsqrt(jnp.sum(widened * widened, axis=-1, keepdims=True) + epsilon)
    ).astype(jnp.bfloat16)
    logits = logit_scale * contract_rows(query_unit, d_ref[...])
    weights = jnp.exp(logits)
    totals = jnp.sum(weights, axis=1, keepdims=True)
    hits = hit_ref[...].astype(jnp.float32)
    chosen_logit = jnp.sum(hits * logits, axis=1, keepdims=True)
    loss_ref[...] = jnp.log(totals) - chosen_logit
    wb_ref[...] = weights.astype(jnp.bfloat16)
    tot_ref[...] = totals
    coefficient_t = (weights / totals - hits).T.astype(jnp.bfloat16)
    acc_ref[...] += logit_scale * jnp.dot(
        coefficient_t, query_unit, preferred_element_type=jnp.float32
    )

    @pl.when(pl.program_id(0) == pl.num_programs(0) - 1)
    def _():
        gd_ref[...] = acc_ref[...].astype(jnp.bfloat16)


def query_grad_kernel(wb_ref, tot_ref, hit_ref, d_ref, gq_ref):
    docs = d_ref[...]
    numerator = jnp.dot(wb_ref[...], docs, preferred_element_type=jnp.float32)
    chosen_doc = jnp.dot(hit_ref[...], docs, preferred_element_type=jnp.float32)
    gq_ref[...] = (logit_scale * (numerator / tot_ref[...] - chosen_doc)).astype(jnp.bfloat16)


def scores(queries, doc_piece, hits, tile=128):
    rows, width = queries.shape
    docs = doc_piece.shape[0]
    return pl.pallas_call(
        score_kernel,
        grid=(rows // tile,),
        in_specs=[
            pl.BlockSpec((tile, width), lambda i: (i, 0)),
            pl.BlockSpec((docs, width), lambda i: (0, 0)),
            pl.BlockSpec((tile, docs), lambda i: (i, 0)),
        ],
        out_specs=[
            pl.BlockSpec((tile, 1), lambda i: (i, 0)),
            pl.BlockSpec((tile, docs), lambda i: (i, 0)),
            pl.BlockSpec((tile, 1), lambda i: (i, 0)),
            pl.BlockSpec((docs, width), lambda i: (0, 0)),
        ],
        out_shape=[
            jax.ShapeDtypeStruct((rows, 1), jnp.float32),
            jax.ShapeDtypeStruct((rows, docs), jnp.bfloat16),
            jax.ShapeDtypeStruct((rows, 1), jnp.float32),
            jax.ShapeDtypeStruct((docs, width), jnp.bfloat16),
        ],
        scratch_shapes=[pltpu.VMEM((docs, width), jnp.float32)],
        compiler_params=pltpu.CompilerParams(dimension_semantics=("arbitrary",)),
        cost_estimate=pl.CostEstimate(
            flops=4 * rows * docs * width, transcendentals=rows * docs, bytes_accessed=2 * rows * width
        ),
    )(queries, doc_piece, hits)


def query_grads(weights, totals, hits, doc_piece, tile=128):
    rows, docs = weights.shape
    width = doc_piece.shape[1]
    return pl.pallas_call(
        query_grad_kernel,
        grid=(rows // tile,),
        in_specs=[
            pl.BlockSpec((tile, docs), lambda i: (i, 0)),
            pl.BlockSpec((tile, 1), lambda i: (i, 0)),
            pl.BlockSpec((tile, docs), lambda i: (i, 0)),
            pl.BlockSpec((docs, width), lambda i: (0, 0)),
        ],
        out_specs=pl.BlockSpec((tile, width), lambda i: (i, 0)),
        out_shape=jax.ShapeDtypeStruct((rows, width), jnp.bfloat16),
        compiler_params=pltpu.CompilerParams(dimension_semantics=("arbitrary",)),
        cost_estimate=pl.CostEstimate(
            flops=4 * rows * docs * width, transcendentals=0, bytes_accessed=2 * rows * width
        ),
    )(weights, totals, hits, doc_piece)


def on_device(
    spans, span_counts, session_ids, destinations, expert_weight, norm_gain, queries, positives
):
    rows_dev = spans.shape[0]
    hidden_width = spans.shape[1]
    groups = lax.axis_size("dp")
    capacity = (rows_dev - 3 * SESS_DEV) // groups
    received = rows_dev // 4
    cycle = rows_dev // groups
    count = span_counts[0]

    lane_of = (jnp.arange(groups, dtype=jnp.int32) - destinations[0]) % groups
    by_lane = spans.reshape(cycle, groups, hidden_width)
    send_rows = jnp.swapaxes(jnp.take(by_lane, lane_of, axis=1, mode="clip"), 0, 1)[
        :, :capacity
    ]
    row_of = lane_of[:, None] + groups * jnp.arange(capacity, dtype=jnp.int32)[None, :]
    ids_by_lane = session_ids.reshape(cycle, groups)
    send_ids = jnp.where(
        row_of < count, jnp.swapaxes(jnp.take(ids_by_lane, lane_of, axis=1, mode="clip"), 0, 1)[:, :capacity], -1
    )
    got_rows = lax.all_to_all(send_rows, "dp", split_axis=0, concat_axis=0, tiled=True)
    got_ids = lax.all_to_all(send_ids, "dp", split_axis=0, concat_axis=0, tiled=True)

    got_counts = jnp.sum((got_ids >= 0).astype(jnp.int32), axis=1)
    starts = jnp.cumsum(got_counts) - got_counts
    packed_index = jnp.arange(received, dtype=jnp.int32)
    source_of = (
        jnp.sum((starts[None, :] <= packed_index[:, None]).astype(jnp.int32), axis=1) - 1
    )
    slot_of = source_of * capacity + packed_index - starts[source_of]
    packed_live = packed_index < jnp.sum(got_counts)
    slot_of = jnp.where(packed_live, slot_of, 0)
    packer = (
        (jnp.arange(groups, dtype=jnp.int32)[None, :, None] == source_of[:, None, None])
        & (jnp.arange(capacity, dtype=jnp.int32)[None, None, :] == (packed_index - starts[source_of])[:, None, None])
        & packed_live[:, None, None]
    ).astype(jnp.bfloat16)
    packed = lax.dot_general(
        packer, got_rows, (((1, 2), (0, 1)), ((), ())), preferred_element_type=jnp.float32
    ).astype(jnp.bfloat16)
    packed_key = jnp.where(
        packed_live, source_of * SESS_DEV + got_ids.reshape(groups * capacity)[slot_of], -1
    )

    widened = packed.astype(jnp.float32)
    normed = (
        widened
        * lax.rsqrt(jnp.mean(widened * widened, axis=-1, keepdims=True) + epsilon)
        * norm_gain
    ).astype(jnp.bfloat16)
    embedded = jax.nn.gelu(
        jnp.dot(normed, expert_weight[0], preferred_element_type=jnp.float32), approximate=True
    ).astype(jnp.bfloat16)
    emb_width = embedded.shape[1]
    selector = (
        jnp.arange(groups * SESS_DEV, dtype=jnp.int32)[:, None] == packed_key[None, :]
    ).astype(jnp.bfloat16)
    partial = jnp.dot(selector, embedded, preferred_element_type=jnp.float32)
    partial = partial.astype(jnp.bfloat16).reshape(groups, SESS_DEV, emb_width)
    returned = lax.all_to_all(partial, "dp", split_axis=0, concat_axis=0, tiled=True)
    pooled = jnp.sum(returned.astype(jnp.float32), axis=0)

    doc_unit = unit_rows(pooled)
    cycle_size = lax.axis_size("blk")
    position = lax.axis_index("blk")
    arrived = jnp.stack(
        [doc_unit]
        + [
            lax.ppermute(doc_unit, "blk", [(i, (i + shift) % cycle_size) for i in range(cycle_size)])
            for shift in range(1, cycle_size)
        ]
    )
    arrival_of = (position - jnp.arange(cycle_size, dtype=jnp.int32)) % cycle_size
    doc_piece = arrived[arrival_of].reshape(cycle_size * doc_unit.shape[0], emb_width)
    piece_rows = doc_piece.shape[0]
    hits = (positives[:, None] == jnp.arange(piece_rows, dtype=jnp.int32)[None, :]).astype(
        jnp.bfloat16
    )
    loss_col, weights, totals, grad_part = scores(queries, doc_piece, hits)
    grad_terms = lax.all_to_all(
        grad_part.reshape(cycle_size, doc_unit.shape[0], emb_width),
        "blk",
        split_axis=0,
        concat_axis=0,
        tiled=True,
    )
    grad_docs = jnp.sum(grad_terms.astype(jnp.float32), axis=0)
    grad_queries = query_grads(weights, totals, hits, doc_piece)
    loss_rows = loss_col.reshape(loss_col.shape[0])
    return (loss_rows, grad_queries, grad_docs)


def solution(mesh):
    placed = (
        P(("dp", "blk"), None),
        P(("dp", "blk")),
        P(("dp", "blk")),
        P(("dp", "blk")),
        P("dp", None, None),
        P(),
        P(("dp", "blk"), None),
        P(("dp", "blk")),
    )
    return jax.shard_map(
        on_device,
        mesh=mesh,
        in_specs=placed,
        out_specs=(P(("dp", "blk")), P(("dp", "blk"), None), P(("dp", "blk"), None)),
        check_vma=False,
    )
```

```python
import jax
import jax.numpy as jnp
from jax import lax
from jax.experimental import pallas as pl
from jax.experimental.pallas import tpu as pltpu
from jax.sharding import PartitionSpec as P

SESS_DEV = 16


logit_scale = 20.0
epsilon = 1e-06


def unit_rows(values):
    widened = values.astype(jnp.float32)
    return (
        widened * lax.rsqrt(jnp.sum(widened * widened, axis=-1, keepdims=True) + epsilon)
    ).astype(jnp.bfloat16)


def contract_rows(left_side, right_side):
    return lax.dot_general(
        left_side, right_side, (((1,), (1,)), ((), ())), preferred_element_type=jnp.float32
    )


def contract_first(left_side, right_side):
    return lax.dot_general(
        left_side, right_side, (((0,), (0,)), ((), ())), preferred_element_type=jnp.float32
    )


def score_kernel(q_ref, d_ref, hit_ref, loss_ref, wb_ref, tot_ref, gd_ref, acc_ref):
    @pl.when(pl.program_id(0) == 0)
    def _():
        acc_ref[...] = jnp.zeros_like(acc_ref)

    query_unit = q_ref[...]
    logits = logit_scale * contract_rows(query_unit, d_ref[...])
    weights = jnp.exp(logits)
    totals = jnp.sum(weights, axis=1, keepdims=True)
    hits = hit_ref[...].astype(jnp.float32)
    chosen_logit = jnp.sum(hits * logits, axis=1, keepdims=True)
    loss_ref[...] = jnp.log(totals) - chosen_logit
    wb_ref[...] = weights.astype(jnp.bfloat16)
    tot_ref[...] = totals
    coefficient_t = (weights / totals - hits).T.astype(jnp.bfloat16)
    acc_ref[...] += logit_scale * jnp.dot(
        coefficient_t, query_unit, preferred_element_type=jnp.float32
    )

    @pl.when(pl.program_id(0) == pl.num_programs(0) - 1)
    def _():
        gd_ref[...] = acc_ref[...].astype(jnp.bfloat16)


def unit_query_kernel(q_ref, qu_ref):
    widened = q_ref[...].astype(jnp.float32)
    qu_ref[...] = (
        widened * lax.rsqrt(jnp.sum(widened * widened, axis=-1, keepdims=True) + epsilon)
    ).astype(jnp.bfloat16)


def unit_queries(queries, tile=128):
    rows, width = queries.shape
    return pl.pallas_call(
        unit_query_kernel,
        grid=(rows // tile,),
        in_specs=[pl.BlockSpec((tile, width), lambda i: (i, 0))],
        out_specs=pl.BlockSpec((tile, width), lambda i: (i, 0)),
        out_shape=jax.ShapeDtypeStruct((rows, width), jnp.bfloat16),
        cost_estimate=pl.CostEstimate(
            flops=4 * rows * width, transcendentals=rows, bytes_accessed=4 * rows * width
        ),
    )(queries)


def query_grad_kernel(wb_ref, tot_ref, hit_ref, d_ref, gq_ref):
    docs = d_ref[...]
    numerator = jnp.dot(wb_ref[...], docs, preferred_element_type=jnp.float32)
    chosen_doc = jnp.dot(hit_ref[...], docs, preferred_element_type=jnp.float32)
    gq_ref[...] = (logit_scale * (numerator / tot_ref[...] - chosen_doc)).astype(jnp.bfloat16)


def scores(queries, doc_piece, hits, tile=128):
    rows, width = queries.shape
    docs = doc_piece.shape[0]
    return pl.pallas_call(
        score_kernel,
        grid=(rows // tile,),
        in_specs=[
            pl.BlockSpec((tile, width), lambda i: (i, 0)),
            pl.BlockSpec((docs, width), lambda i: (0, 0)),
            pl.BlockSpec((tile, docs), lambda i: (i, 0)),
        ],
        out_specs=[
            pl.BlockSpec((tile, 1), lambda i: (i, 0)),
            pl.BlockSpec((tile, docs), lambda i: (i, 0)),
            pl.BlockSpec((tile, 1), lambda i: (i, 0)),
            pl.BlockSpec((docs, width), lambda i: (0, 0)),
        ],
        out_shape=[
            jax.ShapeDtypeStruct((rows, 1), jnp.float32),
            jax.ShapeDtypeStruct((rows, docs), jnp.bfloat16),
            jax.ShapeDtypeStruct((rows, 1), jnp.float32),
            jax.ShapeDtypeStruct((docs, width), jnp.bfloat16),
        ],
        scratch_shapes=[pltpu.VMEM((docs, width), jnp.float32)],
        compiler_params=pltpu.CompilerParams(dimension_semantics=("arbitrary",)),
        cost_estimate=pl.CostEstimate(
            flops=4 * rows * docs * width, transcendentals=rows * docs, bytes_accessed=2 * rows * width
        ),
    )(queries, doc_piece, hits)


def query_grads(weights, totals, hits, doc_piece, tile=128):
    rows, docs = weights.shape
    width = doc_piece.shape[1]
    return pl.pallas_call(
        query_grad_kernel,
        grid=(rows // tile,),
        in_specs=[
            pl.BlockSpec((tile, docs), lambda i: (i, 0)),
            pl.BlockSpec((tile, 1), lambda i: (i, 0)),
            pl.BlockSpec((tile, docs), lambda i: (i, 0)),
            pl.BlockSpec((docs, width), lambda i: (0, 0)),
        ],
        out_specs=pl.BlockSpec((tile, width), lambda i: (i, 0)),
        out_shape=jax.ShapeDtypeStruct((rows, width), jnp.bfloat16),
        compiler_params=pltpu.CompilerParams(dimension_semantics=("arbitrary",)),
        cost_estimate=pl.CostEstimate(
            flops=4 * rows * docs * width, transcendentals=0, bytes_accessed=2 * rows * width
        ),
    )(weights, totals, hits, doc_piece)


def on_device(
    spans, span_counts, session_ids, destinations, expert_weight, norm_gain, queries, positives
):
    rows_dev = spans.shape[0]
    hidden_width = spans.shape[1]
    groups = lax.axis_size("dp")
    capacity = (rows_dev - 3 * SESS_DEV) // groups
    received = rows_dev // 4
    cycle = rows_dev // groups
    count = span_counts[0]

    lane_of = (jnp.arange(groups, dtype=jnp.int32) - destinations[0]) % groups
    by_lane = spans.reshape(cycle, groups, hidden_width)
    send_rows = jnp.swapaxes(jnp.take(by_lane, lane_of, axis=1, mode="clip"), 0, 1)[
        :, :capacity
    ]
    row_of = lane_of[:, None] + groups * jnp.arange(capacity, dtype=jnp.int32)[None, :]
    ids_by_lane = session_ids.reshape(cycle, groups)
    send_ids = jnp.where(
        row_of < count, jnp.swapaxes(jnp.take(ids_by_lane, lane_of, axis=1, mode="clip"), 0, 1)[:, :capacity], -1
    )
    got_rows = lax.all_to_all(send_rows, "dp", split_axis=0, concat_axis=0, tiled=True)
    got_rows, queries = lax.optimization_barrier((got_rows, queries))
    got_ids = lax.all_to_all(send_ids, "dp", split_axis=0, concat_axis=0, tiled=True)

    got_counts = jnp.sum((got_ids >= 0).astype(jnp.int32), axis=1)
    starts = jnp.cumsum(got_counts) - got_counts
    packed_index = jnp.arange(received, dtype=jnp.int32)
    source_of = (
        jnp.sum((starts[None, :] <= packed_index[:, None]).astype(jnp.int32), axis=1) - 1
    )
    slot_of = source_of * capacity + packed_index - starts[source_of]
    packed_live = packed_index < jnp.sum(got_counts)
    slot_of = jnp.where(packed_live, slot_of, 0)
    packer = (
        (jnp.arange(groups, dtype=jnp.int32)[None, :, None] == source_of[:, None, None])
        & (jnp.arange(capacity, dtype=jnp.int32)[None, None, :] == (packed_index - starts[source_of])[:, None, None])
        & packed_live[:, None, None]
    ).astype(jnp.bfloat16)
    packed = lax.dot_general(
        packer, got_rows, (((1, 2), (0, 1)), ((), ())), preferred_element_type=jnp.float32
    ).astype(jnp.bfloat16)
    packed_key = jnp.where(
        packed_live, source_of * SESS_DEV + got_ids.reshape(groups * capacity)[slot_of], -1
    )

    widened = packed.astype(jnp.float32)
    normed = (
        widened
        * lax.rsqrt(jnp.mean(widened * widened, axis=-1, keepdims=True) + epsilon)
        * norm_gain
    ).astype(jnp.bfloat16)
    embedded = jax.nn.gelu(
        jnp.dot(normed, expert_weight[0], preferred_element_type=jnp.float32), approximate=True
    ).astype(jnp.bfloat16)
    emb_width = embedded.shape[1]
    selector = (
        jnp.arange(groups * SESS_DEV, dtype=jnp.int32)[:, None] == packed_key[None, :]
    ).astype(jnp.bfloat16)
    partial = jnp.dot(selector, embedded, preferred_element_type=jnp.float32)
    partial = partial.astype(jnp.bfloat16).reshape(groups, SESS_DEV, emb_width)
    returned = lax.all_to_all(partial, "dp", split_axis=0, concat_axis=0, tiled=True)
    pooled = jnp.sum(returned.astype(jnp.float32), axis=0)

    doc_unit = unit_rows(pooled)
    query_unit = unit_queries(queries)
    cycle_size = lax.axis_size("blk")
    position = lax.axis_index("blk")
    arrived = jnp.stack(
        [doc_unit]
        + [
            lax.ppermute(doc_unit, "blk", [(i, (i + shift) % cycle_size) for i in range(cycle_size)])
            for shift in range(1, cycle_size)
        ]
    )
    arrival_of = (position - jnp.arange(cycle_size, dtype=jnp.int32)) % cycle_size
    doc_piece = arrived[arrival_of].reshape(cycle_size * doc_unit.shape[0], emb_width)
    piece_rows = doc_piece.shape[0]
    hits = (positives[:, None] == jnp.arange(piece_rows, dtype=jnp.int32)[None, :]).astype(
        jnp.bfloat16
    )
    loss_col, weights, totals, grad_part = scores(query_unit, doc_piece, hits)
    grad_terms = lax.all_to_all(
        grad_part.reshape(cycle_size, doc_unit.shape[0], emb_width),
        "blk",
        split_axis=0,
        concat_axis=0,
        tiled=True,
    )
    grad_docs = jnp.sum(grad_terms.astype(jnp.float32), axis=0)
    grad_queries = query_grads(weights, totals, hits, doc_piece)
    loss_rows = loss_col.reshape(loss_col.shape[0])
    return (loss_rows, grad_queries, grad_docs)


def solution(mesh):
    placed = (
        P(("dp", "blk"), None),
        P(("dp", "blk")),
        P(("dp", "blk")),
        P(("dp", "blk")),
        P("dp", None, None),
        P(),
        P(("dp", "blk"), None),
        P(("dp", "blk")),
    )
    return jax.shard_map(
        on_device,
        mesh=mesh,
        in_specs=placed,
        out_specs=(P(("dp", "blk")), P(("dp", "blk"), None), P(("dp", "blk"), None)),
        check_vma=False,
    )
```

```python
import jax
import jax.numpy as jnp
from jax import lax
from jax.experimental import pallas as pl
from jax.experimental.pallas import tpu as pltpu
from jax.sharding import PartitionSpec as P

SESS_DEV = 16


logit_scale = 20.0
epsilon = 1e-06


def unit_rows(values):
    widened = values.astype(jnp.float32)
    return (
        widened * lax.rsqrt(jnp.sum(widened * widened, axis=-1, keepdims=True) + epsilon)
    ).astype(jnp.bfloat16)


def contract_rows(left_side, right_side):
    return lax.dot_general(
        left_side, right_side, (((1,), (1,)), ((), ())), preferred_element_type=jnp.float32
    )


def contract_first(left_side, right_side):
    return lax.dot_general(
        left_side, right_side, (((0,), (0,)), ((), ())), preferred_element_type=jnp.float32
    )


def score_kernel(q_ref, d_ref, hit_ref, loss_ref, wb_ref, tot_ref, gd_ref, acc_ref):
    @pl.when(pl.program_id(0) == 0)
    def _():
        acc_ref[...] = jnp.zeros_like(acc_ref)

    query_unit = q_ref[...]
    logits = logit_scale * contract_rows(query_unit, d_ref[...])
    weights = jnp.exp(logits)
    totals = jnp.sum(weights, axis=1, keepdims=True)
    hits = hit_ref[...].astype(jnp.float32)
    chosen_logit = jnp.sum(hits * logits, axis=1, keepdims=True)
    loss_ref[...] = jnp.log(totals) - chosen_logit
    wb_ref[...] = weights.astype(jnp.bfloat16)
    tot_ref[...] = totals
    coefficient_t = (weights / totals - hits).T.astype(jnp.bfloat16)
    acc_ref[...] += logit_scale * jnp.dot(
        coefficient_t, query_unit, preferred_element_type=jnp.float32
    )

    @pl.when(pl.program_id(0) == pl.num_programs(0) - 1)
    def _():
        gd_ref[...] = acc_ref[...].astype(jnp.bfloat16)


def unit_query_kernel(q_ref, qu_ref):
    widened = q_ref[...].astype(jnp.float32)
    qu_ref[...] = (
        widened * lax.rsqrt(jnp.sum(widened * widened, axis=-1, keepdims=True) + epsilon)
    ).astype(jnp.bfloat16)


def unit_queries(queries, tile=128):
    rows, width = queries.shape
    return pl.pallas_call(
        unit_query_kernel,
        grid=(rows // tile,),
        in_specs=[pl.BlockSpec((tile, width), lambda i: (i, 0))],
        out_specs=pl.BlockSpec((tile, width), lambda i: (i, 0)),
        out_shape=jax.ShapeDtypeStruct((rows, width), jnp.bfloat16),
        cost_estimate=pl.CostEstimate(
            flops=4 * rows * width, transcendentals=rows, bytes_accessed=4 * rows * width
        ),
    )(queries)


def query_grad_kernel(wb_ref, tot_ref, hit_ref, d_ref, gq_ref):
    docs = d_ref[...]
    numerator = jnp.dot(wb_ref[...], docs, preferred_element_type=jnp.float32)
    chosen_doc = jnp.dot(hit_ref[...], docs, preferred_element_type=jnp.float32)
    gq_ref[...] = (logit_scale * (numerator / tot_ref[...] - chosen_doc)).astype(jnp.bfloat16)


def scores(queries, doc_piece, hits, tile=224):
    rows, width = queries.shape
    docs = doc_piece.shape[0]
    return pl.pallas_call(
        score_kernel,
        grid=(rows // tile,),
        in_specs=[
            pl.BlockSpec((tile, width), lambda i: (i, 0)),
            pl.BlockSpec((docs, width), lambda i: (0, 0)),
            pl.BlockSpec((tile, docs), lambda i: (i, 0)),
        ],
        out_specs=[
            pl.BlockSpec((tile, 1), lambda i: (i, 0)),
            pl.BlockSpec((tile, docs), lambda i: (i, 0)),
            pl.BlockSpec((tile, 1), lambda i: (i, 0)),
            pl.BlockSpec((docs, width), lambda i: (0, 0)),
        ],
        out_shape=[
            jax.ShapeDtypeStruct((rows, 1), jnp.float32),
            jax.ShapeDtypeStruct((rows, docs), jnp.bfloat16),
            jax.ShapeDtypeStruct((rows, 1), jnp.float32),
            jax.ShapeDtypeStruct((docs, width), jnp.bfloat16),
        ],
        scratch_shapes=[pltpu.VMEM((docs, width), jnp.float32)],
        compiler_params=pltpu.CompilerParams(dimension_semantics=("arbitrary",)),
        cost_estimate=pl.CostEstimate(
            flops=4 * rows * docs * width, transcendentals=rows * docs, bytes_accessed=2 * rows * width
        ),
    )(queries, doc_piece, hits)


def query_grads(weights, totals, hits, doc_piece, tile=224):
    rows, docs = weights.shape
    width = doc_piece.shape[1]
    return pl.pallas_call(
        query_grad_kernel,
        grid=(rows // tile,),
        in_specs=[
            pl.BlockSpec((tile, docs), lambda i: (i, 0)),
            pl.BlockSpec((tile, 1), lambda i: (i, 0)),
            pl.BlockSpec((tile, docs), lambda i: (i, 0)),
            pl.BlockSpec((docs, width), lambda i: (0, 0)),
        ],
        out_specs=pl.BlockSpec((tile, width), lambda i: (i, 0)),
        out_shape=jax.ShapeDtypeStruct((rows, width), jnp.bfloat16),
        compiler_params=pltpu.CompilerParams(dimension_semantics=("arbitrary",)),
        cost_estimate=pl.CostEstimate(
            flops=4 * rows * docs * width, transcendentals=0, bytes_accessed=2 * rows * width
        ),
    )(weights, totals, hits, doc_piece)


def on_device(
    spans, span_counts, session_ids, destinations, expert_weight, norm_gain, queries, positives
):
    rows_dev = spans.shape[0]
    hidden_width = spans.shape[1]
    groups = lax.axis_size("dp")
    capacity = (rows_dev - 3 * SESS_DEV) // groups
    received = rows_dev // 4
    cycle = rows_dev // groups
    count = span_counts[0]

    lane_of = (jnp.arange(groups, dtype=jnp.int32) - destinations[0]) % groups
    by_lane = spans.reshape(cycle, groups, hidden_width)
    send_rows = jnp.swapaxes(jnp.take(by_lane, lane_of, axis=1, mode="clip"), 0, 1)[
        :, :capacity
    ]
    row_of = lane_of[:, None] + groups * jnp.arange(capacity, dtype=jnp.int32)[None, :]
    ids_by_lane = session_ids.reshape(cycle, groups)
    send_ids = jnp.where(
        row_of < count, jnp.swapaxes(jnp.take(ids_by_lane, lane_of, axis=1, mode="clip"), 0, 1)[:, :capacity], -1
    )
    got_rows = lax.all_to_all(send_rows, "dp", split_axis=0, concat_axis=0, tiled=True)
    got_rows, queries = lax.optimization_barrier((got_rows, queries))
    got_ids = lax.all_to_all(send_ids, "dp", split_axis=0, concat_axis=0, tiled=True)

    got_counts = jnp.sum((got_ids >= 0).astype(jnp.int32), axis=1)
    starts = jnp.cumsum(got_counts) - got_counts
    packed_index = jnp.arange(received, dtype=jnp.int32)
    source_of = (
        jnp.sum((starts[None, :] <= packed_index[:, None]).astype(jnp.int32), axis=1) - 1
    )
    slot_of = source_of * capacity + packed_index - starts[source_of]
    packed_live = packed_index < jnp.sum(got_counts)
    slot_of = jnp.where(packed_live, slot_of, 0)
    packer = (
        (jnp.arange(groups, dtype=jnp.int32)[None, :, None] == source_of[:, None, None])
        & (jnp.arange(capacity, dtype=jnp.int32)[None, None, :] == (packed_index - starts[source_of])[:, None, None])
        & packed_live[:, None, None]
    ).astype(jnp.bfloat16)
    packed = lax.dot_general(
        packer, got_rows, (((1, 2), (0, 1)), ((), ())), preferred_element_type=jnp.float32
    ).astype(jnp.bfloat16)
    packed_key = jnp.where(
        packed_live, source_of * SESS_DEV + got_ids.reshape(groups * capacity)[slot_of], -1
    )

    widened = packed.astype(jnp.float32)
    normed = (
        widened
        * lax.rsqrt(jnp.mean(widened * widened, axis=-1, keepdims=True) + epsilon)
        * norm_gain
    ).astype(jnp.bfloat16)
    embedded = jax.nn.gelu(
        jnp.dot(normed, expert_weight[0], preferred_element_type=jnp.float32), approximate=True
    ).astype(jnp.bfloat16)
    emb_width = embedded.shape[1]
    selector = (
        jnp.arange(groups * SESS_DEV, dtype=jnp.int32)[:, None] == packed_key[None, :]
    ).astype(jnp.bfloat16)
    partial = jnp.dot(selector, embedded, preferred_element_type=jnp.float32)
    partial = partial.astype(jnp.bfloat16).reshape(groups, SESS_DEV, emb_width)
    returned = lax.all_to_all(partial, "dp", split_axis=0, concat_axis=0, tiled=True)
    pooled = jnp.sum(returned.astype(jnp.float32), axis=0)

    doc_unit = unit_rows(pooled)
    query_unit = unit_queries(queries)
    cycle_size = lax.axis_size("blk")
    position = lax.axis_index("blk")
    arrived = jnp.stack(
        [doc_unit]
        + [
            lax.ppermute(doc_unit, "blk", [(i, (i + shift) % cycle_size) for i in range(cycle_size)])
            for shift in range(1, cycle_size)
        ]
    )
    arrival_of = (position - jnp.arange(cycle_size, dtype=jnp.int32)) % cycle_size
    doc_piece = arrived[arrival_of].reshape(cycle_size * doc_unit.shape[0], emb_width)
    piece_rows = doc_piece.shape[0]
    hits = (positives[:, None] == jnp.arange(piece_rows, dtype=jnp.int32)[None, :]).astype(
        jnp.bfloat16
    )
    loss_col, weights, totals, grad_part = scores(query_unit, doc_piece, hits)
    grad_terms = lax.all_to_all(
        grad_part.reshape(cycle_size, doc_unit.shape[0], emb_width),
        "blk",
        split_axis=0,
        concat_axis=0,
        tiled=True,
    )
    grad_docs = jnp.sum(grad_terms.astype(jnp.float32), axis=0)
    grad_queries = query_grads(weights, totals, hits, doc_piece)
    loss_rows = loss_col.reshape(loss_col.shape[0])
    return (loss_rows, grad_queries, grad_docs)


def solution(mesh):
    placed = (
        P(("dp", "blk"), None),
        P(("dp", "blk")),
        P(("dp", "blk")),
        P(("dp", "blk")),
        P("dp", None, None),
        P(),
        P(("dp", "blk"), None),
        P(("dp", "blk")),
    )
    return jax.shard_map(
        on_device,
        mesh=mesh,
        in_specs=placed,
        out_specs=(P(("dp", "blk")), P(("dp", "blk"), None), P(("dp", "blk"), None)),
        check_vma=False,
    )
```

```python
import jax
import jax.numpy as jnp
from jax import lax
from jax.experimental import pallas as pl
from jax.experimental.pallas import tpu as pltpu
from jax.sharding import PartitionSpec as P

SESS_DEV = 16


logit_scale = 20.0
epsilon = 1e-06


def unit_rows(values):
    widened = values.astype(jnp.float32)
    return (
        widened * lax.rsqrt(jnp.sum(widened * widened, axis=-1, keepdims=True) + epsilon)
    ).astype(jnp.bfloat16)


def contract_rows(left_side, right_side):
    return lax.dot_general(
        left_side, right_side, (((1,), (1,)), ((), ())), preferred_element_type=jnp.float32
    )


def contract_first(left_side, right_side):
    return lax.dot_general(
        left_side, right_side, (((0,), (0,)), ((), ())), preferred_element_type=jnp.float32
    )


def score_kernel(q_ref, d_ref, hit_ref, loss_ref, wb_ref, tot_ref, gd_ref, acc_ref):
    @pl.when(pl.program_id(0) == 0)
    def _():
        acc_ref[...] = jnp.zeros_like(acc_ref)

    query_unit = q_ref[...]
    logits = logit_scale * contract_rows(query_unit, d_ref[...])
    weights = jnp.exp(logits)
    totals = jnp.sum(weights, axis=1, keepdims=True)
    hits = hit_ref[...].astype(jnp.float32)
    chosen_logit = jnp.sum(hits * logits, axis=1, keepdims=True)
    loss_ref[...] = jnp.log(totals) - chosen_logit
    wb_ref[...] = weights.astype(jnp.bfloat16)
    tot_ref[...] = totals
    coefficient_t = (weights / totals - hits).T.astype(jnp.bfloat16)
    acc_ref[...] += logit_scale * jnp.dot(
        coefficient_t, query_unit, preferred_element_type=jnp.float32
    )

    @pl.when(pl.program_id(0) == pl.num_programs(0) - 1)
    def _():
        gd_ref[...] = acc_ref[...].astype(jnp.bfloat16)


def unit_query_kernel(q_ref, qu_ref):
    widened = q_ref[...].astype(jnp.float32)
    qu_ref[...] = (
        widened * lax.rsqrt(jnp.sum(widened * widened, axis=-1, keepdims=True) + epsilon)
    ).astype(jnp.bfloat16)


def unit_queries(queries, tile=128):
    rows, width = queries.shape
    return pl.pallas_call(
        unit_query_kernel,
        grid=(rows // tile,),
        in_specs=[pl.BlockSpec((tile, width), lambda i: (i, 0))],
        out_specs=pl.BlockSpec((tile, width), lambda i: (i, 0)),
        out_shape=jax.ShapeDtypeStruct((rows, width), jnp.bfloat16),
        cost_estimate=pl.CostEstimate(
            flops=4 * rows * width, transcendentals=rows, bytes_accessed=4 * rows * width
        ),
    )(queries)


def query_grad_kernel(wb_ref, tot_ref, hit_ref, d_ref, gq_ref):
    docs = d_ref[...]
    numerator = jnp.dot(wb_ref[...], docs, preferred_element_type=jnp.float32)
    chosen_doc = jnp.dot(hit_ref[...], docs, preferred_element_type=jnp.float32)
    gq_ref[...] = (logit_scale * (numerator / tot_ref[...] - chosen_doc)).astype(jnp.bfloat16)


def scores(queries, doc_piece, hits, tile=448):
    rows, width = queries.shape
    docs = doc_piece.shape[0]
    return pl.pallas_call(
        score_kernel,
        grid=(rows // tile,),
        in_specs=[
            pl.BlockSpec((tile, width), lambda i: (i, 0)),
            pl.BlockSpec((docs, width), lambda i: (0, 0)),
            pl.BlockSpec((tile, docs), lambda i: (i, 0)),
        ],
        out_specs=[
            pl.BlockSpec((tile, 1), lambda i: (i, 0)),
            pl.BlockSpec((tile, docs), lambda i: (i, 0)),
            pl.BlockSpec((tile, 1), lambda i: (i, 0)),
            pl.BlockSpec((docs, width), lambda i: (0, 0)),
        ],
        out_shape=[
            jax.ShapeDtypeStruct((rows, 1), jnp.float32),
            jax.ShapeDtypeStruct((rows, docs), jnp.bfloat16),
            jax.ShapeDtypeStruct((rows, 1), jnp.float32),
            jax.ShapeDtypeStruct((docs, width), jnp.bfloat16),
        ],
        scratch_shapes=[pltpu.VMEM((docs, width), jnp.float32)],
        compiler_params=pltpu.CompilerParams(dimension_semantics=("arbitrary",)),
        cost_estimate=pl.CostEstimate(
            flops=4 * rows * docs * width, transcendentals=rows * docs, bytes_accessed=2 * rows * width
        ),
    )(queries, doc_piece, hits)


def query_grads(weights, totals, hits, doc_piece, tile=224):
    rows, docs = weights.shape
    width = doc_piece.shape[1]
    return pl.pallas_call(
        query_grad_kernel,
        grid=(rows // tile,),
        in_specs=[
            pl.BlockSpec((tile, docs), lambda i: (i, 0)),
            pl.BlockSpec((tile, 1), lambda i: (i, 0)),
            pl.BlockSpec((tile, docs), lambda i: (i, 0)),
            pl.BlockSpec((docs, width), lambda i: (0, 0)),
        ],
        out_specs=pl.BlockSpec((tile, width), lambda i: (i, 0)),
        out_shape=jax.ShapeDtypeStruct((rows, width), jnp.bfloat16),
        compiler_params=pltpu.CompilerParams(dimension_semantics=("arbitrary",)),
        cost_estimate=pl.CostEstimate(
            flops=4 * rows * docs * width, transcendentals=0, bytes_accessed=2 * rows * width
        ),
    )(weights, totals, hits, doc_piece)


def on_device(
    spans, span_counts, session_ids, destinations, expert_weight, norm_gain, queries, positives
):
    rows_dev = spans.shape[0]
    hidden_width = spans.shape[1]
    groups = lax.axis_size("dp")
    capacity = (rows_dev - 3 * SESS_DEV) // groups
    received = rows_dev // 4
    cycle = rows_dev // groups
    count = span_counts[0]

    lane_of = (jnp.arange(groups, dtype=jnp.int32) - destinations[0]) % groups
    by_lane = spans.reshape(cycle, groups, hidden_width)
    send_rows = jnp.swapaxes(jnp.take(by_lane, lane_of, axis=1, mode="clip"), 0, 1)[
        :, :capacity
    ]
    row_of = lane_of[:, None] + groups * jnp.arange(capacity, dtype=jnp.int32)[None, :]
    ids_by_lane = session_ids.reshape(cycle, groups)
    send_ids = jnp.where(
        row_of < count, jnp.swapaxes(jnp.take(ids_by_lane, lane_of, axis=1, mode="clip"), 0, 1)[:, :capacity], -1
    )
    got_rows = lax.all_to_all(send_rows, "dp", split_axis=0, concat_axis=0, tiled=True)
    got_rows, queries = lax.optimization_barrier((got_rows, queries))
    got_ids = lax.all_to_all(send_ids, "dp", split_axis=0, concat_axis=0, tiled=True)

    got_counts = jnp.sum((got_ids >= 0).astype(jnp.int32), axis=1)
    starts = jnp.cumsum(got_counts) - got_counts
    packed_index = jnp.arange(received, dtype=jnp.int32)
    source_of = (
        jnp.sum((starts[None, :] <= packed_index[:, None]).astype(jnp.int32), axis=1) - 1
    )
    slot_of = source_of * capacity + packed_index - starts[source_of]
    packed_live = packed_index < jnp.sum(got_counts)
    slot_of = jnp.where(packed_live, slot_of, 0)
    packer = (
        (jnp.arange(groups, dtype=jnp.int32)[None, :, None] == source_of[:, None, None])
        & (jnp.arange(capacity, dtype=jnp.int32)[None, None, :] == (packed_index - starts[source_of])[:, None, None])
        & packed_live[:, None, None]
    ).astype(jnp.bfloat16)
    packed = lax.dot_general(
        packer, got_rows, (((1, 2), (0, 1)), ((), ())), preferred_element_type=jnp.float32
    ).astype(jnp.bfloat16)
    packed_key = jnp.where(
        packed_live, source_of * SESS_DEV + got_ids.reshape(groups * capacity)[slot_of], -1
    )

    widened = packed.astype(jnp.float32)
    normed = (
        widened
        * lax.rsqrt(jnp.mean(widened * widened, axis=-1, keepdims=True) + epsilon)
        * norm_gain
    ).astype(jnp.bfloat16)
    embedded = jax.nn.gelu(
        jnp.dot(normed, expert_weight[0], preferred_element_type=jnp.float32), approximate=True
    ).astype(jnp.bfloat16)
    emb_width = embedded.shape[1]
    selector = (
        jnp.arange(groups * SESS_DEV, dtype=jnp.int32)[:, None] == packed_key[None, :]
    ).astype(jnp.bfloat16)
    partial = jnp.dot(selector, embedded, preferred_element_type=jnp.float32)
    partial = partial.astype(jnp.bfloat16).reshape(groups, SESS_DEV, emb_width)
    returned = lax.all_to_all(partial, "dp", split_axis=0, concat_axis=0, tiled=True)
    pooled = jnp.sum(returned.astype(jnp.float32), axis=0)

    doc_unit = unit_rows(pooled)
    query_unit = unit_queries(queries)
    cycle_size = lax.axis_size("blk")
    position = lax.axis_index("blk")
    arrived = jnp.stack(
        [doc_unit]
        + [
            lax.ppermute(doc_unit, "blk", [(i, (i + shift) % cycle_size) for i in range(cycle_size)])
            for shift in range(1, cycle_size)
        ]
    )
    arrival_of = (position - jnp.arange(cycle_size, dtype=jnp.int32)) % cycle_size
    doc_piece = arrived[arrival_of].reshape(cycle_size * doc_unit.shape[0], emb_width)
    piece_rows = doc_piece.shape[0]
    hits = (positives[:, None] == jnp.arange(piece_rows, dtype=jnp.int32)[None, :]).astype(
        jnp.bfloat16
    )
    loss_col, weights, totals, grad_part = scores(query_unit, doc_piece, hits)
    grad_terms = lax.all_to_all(
        grad_part.reshape(cycle_size, doc_unit.shape[0], emb_width),
        "blk",
        split_axis=0,
        concat_axis=0,
        tiled=True,
    )
    grad_docs = jnp.sum(grad_terms.astype(jnp.float32), axis=0)
    grad_queries = query_grads(weights, totals, hits, doc_piece)
    loss_rows = loss_col.reshape(loss_col.shape[0])
    return (loss_rows, grad_queries, grad_docs)


def solution(mesh):
    placed = (
        P(("dp", "blk"), None),
        P(("dp", "blk")),
        P(("dp", "blk")),
        P(("dp", "blk")),
        P("dp", None, None),
        P(),
        P(("dp", "blk"), None),
        P(("dp", "blk")),
    )
    return jax.shard_map(
        on_device,
        mesh=mesh,
        in_specs=placed,
        out_specs=(P(("dp", "blk")), P(("dp", "blk"), None), P(("dp", "blk"), None)),
        check_vma=False,
    )
```

```python
import jax
import jax.numpy as jnp
from jax import lax
from jax.experimental import pallas as pl
from jax.experimental.pallas import tpu as pltpu
from jax.sharding import PartitionSpec as P

SESS_DEV = 16


logit_scale = 20.0
epsilon = 1e-06


def unit_rows(values):
    widened = values.astype(jnp.float32)
    return (
        widened * lax.rsqrt(jnp.sum(widened * widened, axis=-1, keepdims=True) + epsilon)
    ).astype(jnp.bfloat16)


def contract_rows(left_side, right_side):
    return lax.dot_general(
        left_side, right_side, (((1,), (1,)), ((), ())), preferred_element_type=jnp.float32
    )


def contract_first(left_side, right_side):
    return lax.dot_general(
        left_side, right_side, (((0,), (0,)), ((), ())), preferred_element_type=jnp.float32
    )


def score_kernel(q_ref, d_ref, hit_ref, loss_ref, wb_ref, tot_ref, gd_ref, acc_ref):
    @pl.when(pl.program_id(0) == 0)
    def _():
        acc_ref[...] = jnp.zeros_like(acc_ref)

    query_unit = q_ref[...]
    logits = logit_scale * contract_rows(query_unit, d_ref[...])
    weights = jnp.exp(logits)
    totals = jnp.sum(weights, axis=1, keepdims=True)
    hits = hit_ref[...].astype(jnp.float32)
    chosen_logit = jnp.sum(hits * logits, axis=1, keepdims=True)
    loss_ref[...] = jnp.log(totals) - chosen_logit
    wb_ref[...] = weights.astype(jnp.bfloat16)
    tot_ref[...] = totals
    coefficient_t = (weights / totals - hits).T.astype(jnp.bfloat16)
    acc_ref[...] += logit_scale * jnp.dot(
        coefficient_t, query_unit, preferred_element_type=jnp.float32
    )

    @pl.when(pl.program_id(0) == pl.num_programs(0) - 1)
    def _():
        pieces = lax.axis_size("blk")
        rows = gd_ref.shape[0] // pieces
        position = lax.axis_index("blk")
        for block in range(pieces):
            slot = lax.rem(position - block + pieces, pieces)
            gd_ref[pl.ds(block * rows, rows), :] = acc_ref[
                pl.ds(pl.multiple_of(slot * rows, rows), rows), :
            ].astype(jnp.bfloat16)


def unit_query_kernel(q_ref, qu_ref):
    widened = q_ref[...].astype(jnp.float32)
    qu_ref[...] = (
        widened * lax.rsqrt(jnp.sum(widened * widened, axis=-1, keepdims=True) + epsilon)
    ).astype(jnp.bfloat16)


def unit_queries(queries, tile=128):
    rows, width = queries.shape
    return pl.pallas_call(
        unit_query_kernel,
        grid=(rows // tile,),
        in_specs=[pl.BlockSpec((tile, width), lambda i: (i, 0))],
        out_specs=pl.BlockSpec((tile, width), lambda i: (i, 0)),
        out_shape=jax.ShapeDtypeStruct((rows, width), jnp.bfloat16),
        cost_estimate=pl.CostEstimate(
            flops=4 * rows * width, transcendentals=rows, bytes_accessed=4 * rows * width
        ),
    )(queries)


def query_grad_kernel(wb_ref, tot_ref, hit_ref, d_ref, gq_ref):
    docs = d_ref[...]
    numerator = jnp.dot(wb_ref[...], docs, preferred_element_type=jnp.float32)
    chosen_doc = jnp.dot(hit_ref[...], docs, preferred_element_type=jnp.float32)
    gq_ref[...] = (logit_scale * (numerator / tot_ref[...] - chosen_doc)).astype(jnp.bfloat16)


def scores(queries, doc_piece, hits, tile=224):
    rows, width = queries.shape
    docs = doc_piece.shape[0]
    return pl.pallas_call(
        score_kernel,
        grid=(rows // tile,),
        in_specs=[
            pl.BlockSpec((tile, width), lambda i: (i, 0)),
            pl.BlockSpec((docs, width), lambda i: (0, 0)),
            pl.BlockSpec((tile, docs), lambda i: (i, 0)),
        ],
        out_specs=[
            pl.BlockSpec((tile, 1), lambda i: (i, 0)),
            pl.BlockSpec((tile, docs), lambda i: (i, 0)),
            pl.BlockSpec((tile, 1), lambda i: (i, 0)),
            pl.BlockSpec((docs, width), lambda i: (0, 0)),
        ],
        out_shape=[
            jax.ShapeDtypeStruct((rows, 1), jnp.float32),
            jax.ShapeDtypeStruct((rows, docs), jnp.bfloat16),
            jax.ShapeDtypeStruct((rows, 1), jnp.float32),
            jax.ShapeDtypeStruct((docs, width), jnp.bfloat16),
        ],
        scratch_shapes=[pltpu.VMEM((docs, width), jnp.float32)],
        compiler_params=pltpu.CompilerParams(dimension_semantics=("arbitrary",)),
        cost_estimate=pl.CostEstimate(
            flops=4 * rows * docs * width, transcendentals=rows * docs, bytes_accessed=2 * rows * width
        ),
    )(queries, doc_piece, hits)


def query_grads(weights, totals, hits, doc_piece, tile=224):
    rows, docs = weights.shape
    width = doc_piece.shape[1]
    return pl.pallas_call(
        query_grad_kernel,
        grid=(rows // tile,),
        in_specs=[
            pl.BlockSpec((tile, docs), lambda i: (i, 0)),
            pl.BlockSpec((tile, 1), lambda i: (i, 0)),
            pl.BlockSpec((tile, docs), lambda i: (i, 0)),
            pl.BlockSpec((docs, width), lambda i: (0, 0)),
        ],
        out_specs=pl.BlockSpec((tile, width), lambda i: (i, 0)),
        out_shape=jax.ShapeDtypeStruct((rows, width), jnp.bfloat16),
        compiler_params=pltpu.CompilerParams(dimension_semantics=("arbitrary",)),
        cost_estimate=pl.CostEstimate(
            flops=4 * rows * docs * width, transcendentals=0, bytes_accessed=2 * rows * width
        ),
    )(weights, totals, hits, doc_piece)


def on_device(
    spans, span_counts, session_ids, destinations, expert_weight, norm_gain, queries, positives
):
    rows_dev = spans.shape[0]
    hidden_width = spans.shape[1]
    groups = lax.axis_size("dp")
    capacity = (rows_dev - 3 * SESS_DEV) // groups
    received = rows_dev // 4
    cycle = rows_dev // groups
    count = span_counts[0]

    lane_of = (jnp.arange(groups, dtype=jnp.int32) - destinations[0]) % groups
    by_lane = spans.reshape(cycle, groups, hidden_width)
    send_rows = jnp.swapaxes(jnp.take(by_lane, lane_of, axis=1, mode="clip"), 0, 1)[
        :, :capacity
    ]
    row_of = lane_of[:, None] + groups * jnp.arange(capacity, dtype=jnp.int32)[None, :]
    ids_by_lane = session_ids.reshape(cycle, groups)
    send_ids = jnp.where(
        row_of < count, jnp.swapaxes(jnp.take(ids_by_lane, lane_of, axis=1, mode="clip"), 0, 1)[:, :capacity], -1
    )
    got_rows = lax.all_to_all(send_rows, "dp", split_axis=0, concat_axis=0, tiled=True)
    got_rows, queries = lax.optimization_barrier((got_rows, queries))
    got_ids = lax.all_to_all(send_ids, "dp", split_axis=0, concat_axis=0, tiled=True)

    got_counts = jnp.sum((got_ids >= 0).astype(jnp.int32), axis=1)
    starts = jnp.cumsum(got_counts) - got_counts
    packed_index = jnp.arange(received, dtype=jnp.int32)
    source_of = (
        jnp.sum((starts[None, :] <= packed_index[:, None]).astype(jnp.int32), axis=1) - 1
    )
    slot_of = source_of * capacity + packed_index - starts[source_of]
    packed_live = packed_index < jnp.sum(got_counts)
    slot_of = jnp.where(packed_live, slot_of, 0)
    packer = (
        (jnp.arange(groups, dtype=jnp.int32)[None, :, None] == source_of[:, None, None])
        & (jnp.arange(capacity, dtype=jnp.int32)[None, None, :] == (packed_index - starts[source_of])[:, None, None])
        & packed_live[:, None, None]
    ).astype(jnp.bfloat16)
    packed = lax.dot_general(
        packer, got_rows, (((1, 2), (0, 1)), ((), ())), preferred_element_type=jnp.float32
    ).astype(jnp.bfloat16)
    packed_key = jnp.where(
        packed_live, source_of * SESS_DEV + got_ids.reshape(groups * capacity)[slot_of], -1
    )

    widened = packed.astype(jnp.float32)
    normed = (
        widened
        * lax.rsqrt(jnp.mean(widened * widened, axis=-1, keepdims=True) + epsilon)
        * norm_gain
    ).astype(jnp.bfloat16)
    embedded = jax.nn.gelu(
        jnp.dot(normed, expert_weight[0], preferred_element_type=jnp.float32), approximate=True
    ).astype(jnp.bfloat16)
    emb_width = embedded.shape[1]
    selector = (
        jnp.arange(groups * SESS_DEV, dtype=jnp.int32)[:, None] == packed_key[None, :]
    ).astype(jnp.bfloat16)
    partial = jnp.dot(selector, embedded, preferred_element_type=jnp.float32)
    partial = partial.astype(jnp.bfloat16).reshape(groups, SESS_DEV, emb_width)
    returned = lax.all_to_all(partial, "dp", split_axis=0, concat_axis=0, tiled=True)
    pooled = jnp.sum(returned.astype(jnp.float32), axis=0)

    doc_unit = unit_rows(pooled)
    query_unit = unit_queries(queries)
    cycle_size = lax.axis_size("blk")
    position = lax.axis_index("blk")
    arrived = jnp.stack(
        [doc_unit]
        + [
            lax.ppermute(doc_unit, "blk", [(i, (i + shift) % cycle_size) for i in range(cycle_size)])
            for shift in range(1, cycle_size)
        ]
    )
    doc_piece = arrived.reshape(cycle_size * doc_unit.shape[0], emb_width)
    piece_rows = doc_piece.shape[0]
    arrival_slot = (position - positives // doc_unit.shape[0]) % cycle_size
    arrival_index = arrival_slot * doc_unit.shape[0] + positives % doc_unit.shape[0]
    hits = (arrival_index[:, None] == jnp.arange(piece_rows, dtype=jnp.int32)[None, :]).astype(
        jnp.bfloat16
    )
    loss_col, weights, totals, grad_part = scores(query_unit, doc_piece, hits)
    grad_terms = lax.all_to_all(
        grad_part.reshape(cycle_size, doc_unit.shape[0], emb_width),
        "blk",
        split_axis=0,
        concat_axis=0,
        tiled=True,
    )
    grad_docs = jnp.sum(grad_terms.astype(jnp.float32), axis=0)
    grad_queries = query_grads(weights, totals, hits, doc_piece)
    loss_rows = loss_col.reshape(loss_col.shape[0])
    return (loss_rows, grad_queries, grad_docs)


def solution(mesh):
    placed = (
        P(("dp", "blk"), None),
        P(("dp", "blk")),
        P(("dp", "blk")),
        P(("dp", "blk")),
        P("dp", None, None),
        P(),
        P(("dp", "blk"), None),
        P(("dp", "blk")),
    )
    return jax.shard_map(
        on_device,
        mesh=mesh,
        in_specs=placed,
        out_specs=(P(("dp", "blk")), P(("dp", "blk"), None), P(("dp", "blk"), None)),
        check_vma=False,
    )
```

```python
import jax
import jax.numpy as jnp
from jax import lax
from jax.experimental import pallas as pl
from jax.experimental.pallas import tpu as pltpu
from jax.sharding import PartitionSpec as P

SESS_DEV = 16


logit_scale = 20.0
epsilon = 1e-06


def unit_rows(values):
    widened = values.astype(jnp.float32)
    return (
        widened * lax.rsqrt(jnp.sum(widened * widened, axis=-1, keepdims=True) + epsilon)
    ).astype(jnp.bfloat16)


def contract_rows(left_side, right_side):
    return lax.dot_general(
        left_side, right_side, (((1,), (1,)), ((), ())), preferred_element_type=jnp.float32
    )


def contract_first(left_side, right_side):
    return lax.dot_general(
        left_side, right_side, (((0,), (0,)), ((), ())), preferred_element_type=jnp.float32
    )


def score_kernel(q_ref, d_ref, hit_ref, loss_ref, wb_ref, tot_ref, gd_ref, acc_ref):
    @pl.when(pl.program_id(0) == 0)
    def _():
        acc_ref[...] = jnp.zeros_like(acc_ref)

    query_unit = q_ref[...]
    logits = logit_scale * contract_rows(query_unit, d_ref[...])
    weights = jnp.exp(logits)
    totals = jnp.sum(weights, axis=1, keepdims=True)
    hits = hit_ref[...].astype(jnp.float32)
    chosen_logit = jnp.sum(hits * logits, axis=1, keepdims=True)
    loss_ref[...] = jnp.log(totals) - chosen_logit
    wb_ref[...] = weights.astype(jnp.bfloat16)
    tot_ref[...] = totals
    coefficient_t = (weights * (1.0 / totals) - hits).T.astype(jnp.bfloat16)
    acc_ref[...] += logit_scale * jnp.dot(
        coefficient_t, query_unit, preferred_element_type=jnp.float32
    )

    @pl.when(pl.program_id(0) == pl.num_programs(0) - 1)
    def _():
        pieces = lax.axis_size("blk")
        rows = gd_ref.shape[0] // pieces
        position = lax.axis_index("blk")
        for block in range(pieces):
            slot = lax.rem(position - block + pieces, pieces)
            gd_ref[pl.ds(block * rows, rows), :] = acc_ref[
                pl.ds(pl.multiple_of(slot * rows, rows), rows), :
            ].astype(jnp.bfloat16)


def unit_query_kernel(q_ref, qu_ref):
    widened = q_ref[...].astype(jnp.float32)
    qu_ref[...] = (
        widened * lax.rsqrt(jnp.sum(widened * widened, axis=-1, keepdims=True) + epsilon)
    ).astype(jnp.bfloat16)


def unit_queries(queries, tile=128):
    rows, width = queries.shape
    return pl.pallas_call(
        unit_query_kernel,
        grid=(rows // tile,),
        in_specs=[pl.BlockSpec((tile, width), lambda i: (i, 0))],
        out_specs=pl.BlockSpec((tile, width), lambda i: (i, 0)),
        out_shape=jax.ShapeDtypeStruct((rows, width), jnp.bfloat16),
        cost_estimate=pl.CostEstimate(
            flops=4 * rows * width, transcendentals=rows, bytes_accessed=4 * rows * width
        ),
    )(queries)


def query_grad_kernel(wb_ref, tot_ref, hit_ref, d_ref, gq_ref):
    docs = d_ref[...]
    numerator = jnp.dot(wb_ref[...], docs, preferred_element_type=jnp.float32)
    chosen_doc = jnp.dot(hit_ref[...], docs, preferred_element_type=jnp.float32)
    gq_ref[...] = (logit_scale * (numerator / tot_ref[...] - chosen_doc)).astype(jnp.bfloat16)


def scores(queries, doc_piece, hits, tile=224):
    rows, width = queries.shape
    docs = doc_piece.shape[0]
    return pl.pallas_call(
        score_kernel,
        grid=(rows // tile,),
        in_specs=[
            pl.BlockSpec((tile, width), lambda i: (i, 0)),
            pl.BlockSpec((docs, width), lambda i: (0, 0)),
            pl.BlockSpec((tile, docs), lambda i: (i, 0)),
        ],
        out_specs=[
            pl.BlockSpec((tile, 1), lambda i: (i, 0)),
            pl.BlockSpec((tile, docs), lambda i: (i, 0)),
            pl.BlockSpec((tile, 1), lambda i: (i, 0)),
            pl.BlockSpec((docs, width), lambda i: (0, 0)),
        ],
        out_shape=[
            jax.ShapeDtypeStruct((rows, 1), jnp.float32),
            jax.ShapeDtypeStruct((rows, docs), jnp.bfloat16),
            jax.ShapeDtypeStruct((rows, 1), jnp.float32),
            jax.ShapeDtypeStruct((docs, width), jnp.bfloat16),
        ],
        scratch_shapes=[pltpu.VMEM((docs, width), jnp.float32)],
        compiler_params=pltpu.CompilerParams(dimension_semantics=("arbitrary",)),
        cost_estimate=pl.CostEstimate(
            flops=4 * rows * docs * width, transcendentals=rows * docs, bytes_accessed=2 * rows * width
        ),
    )(queries, doc_piece, hits)


def query_grads(weights, totals, hits, doc_piece, tile=224):
    rows, docs = weights.shape
    width = doc_piece.shape[1]
    return pl.pallas_call(
        query_grad_kernel,
        grid=(rows // tile,),
        in_specs=[
            pl.BlockSpec((tile, docs), lambda i: (i, 0)),
            pl.BlockSpec((tile, 1), lambda i: (i, 0)),
            pl.BlockSpec((tile, docs), lambda i: (i, 0)),
            pl.BlockSpec((docs, width), lambda i: (0, 0)),
        ],
        out_specs=pl.BlockSpec((tile, width), lambda i: (i, 0)),
        out_shape=jax.ShapeDtypeStruct((rows, width), jnp.bfloat16),
        compiler_params=pltpu.CompilerParams(dimension_semantics=("arbitrary",)),
        cost_estimate=pl.CostEstimate(
            flops=4 * rows * docs * width, transcendentals=0, bytes_accessed=2 * rows * width
        ),
    )(weights, totals, hits, doc_piece)


def on_device(
    spans, span_counts, session_ids, destinations, expert_weight, norm_gain, queries, positives
):
    rows_dev = spans.shape[0]
    hidden_width = spans.shape[1]
    groups = lax.axis_size("dp")
    capacity = (rows_dev - 3 * SESS_DEV) // groups
    received = rows_dev // 4
    cycle = rows_dev // groups
    count = span_counts[0]

    lane_of = (jnp.arange(groups, dtype=jnp.int32) - destinations[0]) % groups
    by_lane = spans.reshape(cycle, groups, hidden_width)
    send_rows = jnp.swapaxes(jnp.take(by_lane, lane_of, axis=1, mode="clip"), 0, 1)[
        :, :capacity
    ]
    row_of = lane_of[:, None] + groups * jnp.arange(capacity, dtype=jnp.int32)[None, :]
    ids_by_lane = session_ids.reshape(cycle, groups)
    send_ids = jnp.where(
        row_of < count, jnp.swapaxes(jnp.take(ids_by_lane, lane_of, axis=1, mode="clip"), 0, 1)[:, :capacity], -1
    )
    got_rows = lax.all_to_all(send_rows, "dp", split_axis=0, concat_axis=0, tiled=True)
    got_rows, queries = lax.optimization_barrier((got_rows, queries))
    got_ids = lax.all_to_all(send_ids, "dp", split_axis=0, concat_axis=0, tiled=True)

    got_counts = jnp.sum((got_ids >= 0).astype(jnp.int32), axis=1)
    starts = jnp.cumsum(got_counts) - got_counts
    packed_index = jnp.arange(received, dtype=jnp.int32)
    source_of = (
        jnp.sum((starts[None, :] <= packed_index[:, None]).astype(jnp.int32), axis=1) - 1
    )
    slot_of = source_of * capacity + packed_index - starts[source_of]
    packed_live = packed_index < jnp.sum(got_counts)
    slot_of = jnp.where(packed_live, slot_of, 0)
    packer = (
        (jnp.arange(groups, dtype=jnp.int32)[None, :, None] == source_of[:, None, None])
        & (jnp.arange(capacity, dtype=jnp.int32)[None, None, :] == (packed_index - starts[source_of])[:, None, None])
        & packed_live[:, None, None]
    ).astype(jnp.bfloat16)
    packed = lax.dot_general(
        packer, got_rows, (((1, 2), (0, 1)), ((), ())), preferred_element_type=jnp.float32
    ).astype(jnp.bfloat16)
    packed_key = jnp.where(
        packed_live, source_of * SESS_DEV + got_ids.reshape(groups * capacity)[slot_of], -1
    )

    widened = packed.astype(jnp.float32)
    normed = (
        widened
        * lax.rsqrt(jnp.mean(widened * widened, axis=-1, keepdims=True) + epsilon)
        * norm_gain
    ).astype(jnp.bfloat16)
    embedded = jax.nn.gelu(
        jnp.dot(normed, expert_weight[0], preferred_element_type=jnp.float32), approximate=True
    ).astype(jnp.bfloat16)
    emb_width = embedded.shape[1]
    selector = (
        jnp.arange(groups * SESS_DEV, dtype=jnp.int32)[:, None] == packed_key[None, :]
    ).astype(jnp.bfloat16)
    partial = jnp.dot(selector, embedded, preferred_element_type=jnp.float32)
    partial = partial.astype(jnp.bfloat16).reshape(groups, SESS_DEV, emb_width)
    returned = lax.all_to_all(partial, "dp", split_axis=0, concat_axis=0, tiled=True)
    pooled = jnp.sum(returned.astype(jnp.float32), axis=0)

    doc_unit = unit_rows(pooled)
    query_unit = unit_queries(queries)
    cycle_size = lax.axis_size("blk")
    position = lax.axis_index("blk")
    arrived = jnp.stack(
        [doc_unit]
        + [
            lax.ppermute(doc_unit, "blk", [(i, (i + shift) % cycle_size) for i in range(cycle_size)])
            for shift in range(1, cycle_size)
        ]
    )
    doc_piece = arrived.reshape(cycle_size * doc_unit.shape[0], emb_width)
    piece_rows = doc_piece.shape[0]
    arrival_slot = (position - positives // doc_unit.shape[0]) % cycle_size
    arrival_index = arrival_slot * doc_unit.shape[0] + positives % doc_unit.shape[0]
    hits = (arrival_index[:, None] == jnp.arange(piece_rows, dtype=jnp.int32)[None, :]).astype(
        jnp.bfloat16
    )
    loss_col, weights, totals, grad_part = scores(query_unit, doc_piece, hits)
    grad_terms = lax.all_to_all(
        grad_part.reshape(cycle_size, doc_unit.shape[0], emb_width),
        "blk",
        split_axis=0,
        concat_axis=0,
        tiled=True,
    )
    grad_docs = jnp.sum(grad_terms.astype(jnp.float32), axis=0)
    grad_queries = query_grads(weights, totals, hits, doc_piece)
    loss_rows = loss_col.reshape(loss_col.shape[0])
    return (loss_rows, grad_queries, grad_docs)


def solution(mesh):
    placed = (
        P(("dp", "blk"), None),
        P(("dp", "blk")),
        P(("dp", "blk")),
        P(("dp", "blk")),
        P("dp", None, None),
        P(),
        P(("dp", "blk"), None),
        P(("dp", "blk")),
    )
    return jax.shard_map(
        on_device,
        mesh=mesh,
        in_specs=placed,
        out_specs=(P(("dp", "blk")), P(("dp", "blk"), None), P(("dp", "blk"), None)),
        check_vma=False,
    )
```
